32 devices in a mesh: groups: 2 (over y), seq: 4 (over z), head: 2 (over x), sub: 2 (over core).
Axes of the slice: x: 2, y: 2, z: 4, core: 2. Of those that a mesh axis runs over, the one named last changes fastest.
Arguments:
- activations: bfloat16 [16384, 1024], P(('groups', 'seq', 'sub')), parts along dimension 0, may hold values from -21 to 21
- w_query: bfloat16 [1024, 1024], P(None, 'head'), may hold values from -0.1875 to 0.1875
- w_key: bfloat16 [1024, 1024], P(None, 'head'), may hold values from -0.1875 to 0.1875
- w_value: bfloat16 [1024, 1024], P(None, 'head'), may hold values from -0.1875 to 0.1875
- w_out: bfloat16 [1024, 1024], P('head'), may hold values from -0.1875 to 0.1875
- tile_lists: int32 [128, 8], P('groups'), parts along dimension 0, may hold values from 0 to 63, as said below
- query_block_counts: int32 [128], P('groups'), parts along dimension 0, may hold values from 4 to 8, as said below
Outputs:
- mixed: bfloat16 [16384, 1024], P(('groups', 'seq', 'sub'), 'head'), parts along dimension 0
The draws below stay inside these ranges and needn't reach their ends.
There are 2 independent parts, one for each index of `groups`. The reference program is written for one: setup_inputs(seed, part) draws one part's arguments, and reference() takes and returns one part's arrays. A program takes and returns all parts, laid end to end along the dimension named above; an argument that names none is the same for every part. Nothing has to cross between parts.
Inputs may be any that keep to these rules, and one draw needn't show every extreme that they name: `tile_lists`: each row lists 8 different key tiles; only its first query_block_counts entries are used. Take the aligned blocks of 8 rows (one device's query blocks) and of 8 tiles (one device's key tiles): the used entries of one block of rows name exactly 4 different tiles of every block of tiles. `query_block_counts`: the last row of each aligned block of 8 rows is 8.
All inputs are finite; a program needn't handle non-finite values.
Results may differ from the reference program's by a relative error of at most 0.019.
The reference program's roundings to bfloat16 on the way count: a program that leaves them out, or rounds other values in their place, can miss the bound.
Values may be sent and summed in bfloat16 or wider, within the bound.
No kernel may reach another device: no remote copies, remote signals or barrier semaphores. Data moves between devices by JAX's collectives and lax.ppermute only.
A program may use at most 128 MiB of HBM per device.

```python
import jax
import jax.numpy as jnp
from jax import lax

H = 8
HS = 128
TILE = 128
MAXT = 8
BALANCING_ROUNDS = 3
QB_DEV = 8
D = 1024
NQB = 64
SEQ_LEN = 8192
CAP = 4
N_SEQ = 4
N_SUB = 2


def draw_activations(key, part):
    key_base = jax.random.fold_in(key, 0)
    return jnp.clip(jax.random.normal(key_base, (SEQ_LEN, D), jnp.float32), -6.0, 6.0).astype(jnp.bfloat16)


def draw_tile_lists(key, part):
    seq_devices = N_SEQ * N_SUB
    cand_count = seq_devices * CAP
    key_sets, key_order = jax.random.split(key, 2)
    pair_keys = jax.random.split(key_sets, seq_devices * seq_devices)
    local_ids = jax.vmap(lambda subkey: jax.random.permutation(subkey, QB_DEV))(pair_keys)[:, :CAP]
    local_ids = local_ids.reshape(seq_devices, seq_devices, CAP).astype(jnp.int32)
    owners = jnp.arange(seq_devices, dtype=jnp.int32)[None, :, None]
    candidates = (owners * QB_DEV + local_ids).reshape(seq_devices, cand_count)
    order_keys = jax.random.split(key_order, seq_devices)
    orders = jax.vmap(lambda subkey: jax.random.permutation(subkey, cand_count))(order_keys).astype(jnp.int32)
    position = (jnp.arange(QB_DEV, dtype=jnp.int32)[:, None] * (MAXT // 2) + jnp.arange(MAXT, dtype=jnp.int32)[None, :]) % cand_count
    picked = orders[:, position.reshape(-1)]
    picked_tiles = jnp.take_along_axis(candidates, picked, axis=1)
    return picked_tiles.reshape(NQB, MAXT).astype(jnp.int32)


def draw_query_block_counts(key, part):
    entry_counts = jax.random.randint(key, (NQB,), MAXT // 2, MAXT + 1, dtype=jnp.int32)
    last_row = jnp.arange(NQB, dtype=jnp.int32) % QB_DEV == QB_DEV - 1
    return jnp.where(last_row, MAXT, entry_counts).astype(jnp.int32)


def block_scale(rng, extent, shards, smallest, high):
    gain, own = 1.0, jax.random.fold_in(rng, 6)
    for dim, shards_of in shards:
        draws = jnp.exp(jax.random.uniform(jax.random.fold_in(own, dim), (shards_of,), jnp.float32, smallest / len(shards), high / len(shards)))
        gain = gain * jnp.repeat(draws, extent[dim] // shards_of).reshape([-1 if axis == dim else 1 for axis in range(len(extent))])
    return gain


def noise(rng, dims, deviation, bound, cuts=(), kind=jnp.bfloat16):
    result = deviation * jax.random.normal(rng, dims, jnp.float32)
    if cuts:
        result = result * block_scale(rng, dims, cuts, -0.22, 0.18)
    return jnp.clip(result, -bound, bound).astype(kind)


def setup_inputs(seed: int = 0, part: int = 0) -> dict:
    keys = jax.random.split(jax.random.key(seed), 8)
    own_keys = jax.random.split(jax.random.fold_in(keys[7], part), 8)
    return {
        "activations": draw_activations(jax.random.fold_in(jax.random.fold_in(keys[7], part), 71), part),
        "w_query": noise(keys[1], (D, D), D ** -0.5, 0.1875, ((1, 2),)),
        "w_key": noise(keys[2], (D, D), D ** -0.5, 0.1875, ((1, 2),)),
        "w_value": noise(keys[3], (D, D), D ** -0.5, 0.1875, ((1, 2),)),
        "w_out": noise(keys[4], (D, D), D ** -0.5, 0.1875, ((0, 2),)),
        "tile_lists": draw_tile_lists(jax.random.fold_in(jax.random.fold_in(keys[7], part), 71), part),
        "query_block_counts": draw_query_block_counts(jax.random.fold_in(jax.random.fold_in(keys[7], part), 71), part),
    }


COLUMN_FLOOR = 0.1


def reference(activations, w_query, w_key, w_value, w_out, tile_lists, query_block_counts):
    query_rows = jnp.dot(activations, w_query, preferred_element_type=jnp.float32).astype(jnp.bfloat16)
    key_proj = jnp.dot(activations, w_key, preferred_element_type=jnp.float32).astype(jnp.bfloat16)
    values = jnp.dot(activations, w_value, preferred_element_type=jnp.float32).astype(jnp.bfloat16)
    valid_slots = jnp.arange(MAXT, dtype=jnp.int32)[None, :] < query_block_counts[:, None]
    onehot = ((tile_lists[:, :, None] == jnp.arange(NQB, dtype=jnp.int32)[None, None, :]) & valid_slots[:, :, None]).astype(jnp.float32)
    valid_mask = valid_slots[:, None, :, None]

    def split_heads(stacked):
        return stacked.reshape(NQB, TILE, H, HS).transpose(2, 0, 1, 3)

    def one_head(operands):
        head_q, head_k, head_v = operands
        key_slots = head_k[tile_lists].astype(jnp.float32)
        value_slots = head_v[tile_lists].astype(jnp.float32)
        scores = jnp.einsum('bid,bmjd->bimj', head_q.astype(jnp.float32), key_slots, precision=lax.Precision.HIGHEST) * (HS ** -0.5)
        row_max = jnp.max(jnp.where(valid_mask, scores, -1e30), axis=(2, 3), keepdims=True)
        weights = jnp.where(valid_mask, jnp.exp(scores - row_max), 0.0)
        for round_number in range(BALANCING_ROUNDS):
            weights = weights / jnp.sum(weights, axis=(2, 3), keepdims=True)
            partial_cols = jnp.sum(weights, axis=1)
            totals = jnp.einsum('bmt,bmj->tj', onehot, partial_cols, precision=lax.Precision.HIGHEST)
            per_slot = jnp.einsum('bmt,tj->bmj', onehot, totals, precision=lax.Precision.HIGHEST)
            weights = weights / jnp.maximum(per_slot[:, None, :, :], COLUMN_FLOOR)
        probabilities = weights.astype(jnp.bfloat16)
        attended = jnp.einsum('bimj,bmjd->bid', probabilities.astype(jnp.float32), value_slots, precision=lax.Precision.HIGHEST)
        return attended.astype(jnp.bfloat16)

    head_outputs = lax.map(one_head, (split_heads(query_rows), split_heads(key_proj), split_heads(values)))
    joined = head_outputs.transpose(1, 2, 0, 3).reshape(SEQ_LEN, H * HS)
    return jnp.dot(joined, w_out, preferred_element_type=jnp.float32).astype(jnp.bfloat16)
```

```python
import jax
import jax.numpy as jnp
from jax import lax
from jax.sharding import PartitionSpec as P

HS = 128
TILE = 128
BALANCING_ROUNDS = 3


COLUMN_FLOOR = 0.1


def body(activations, w_query, w_key, w_value, w_out, tile_lists, query_block_counts):
    seq_devices = lax.axis_size(("seq", "sub"))
    device_index = lax.axis_index(("seq", "sub"))
    block_total = tile_lists.shape[0]
    maximum_tiles = tile_lists.shape[1]
    row_count = activations.shape[0]
    local_blocks = row_count // TILE
    heads_here = w_query.shape[1] // HS
    capacity = local_blocks * (maximum_tiles // 2) // seq_devices
    query_rows = jnp.dot(activations, w_query, preferred_element_type=jnp.float32).astype(
        jnp.bfloat16
    )
    key_proj = jnp.dot(activations, w_key, preferred_element_type=jnp.float32).astype(jnp.bfloat16)
    values = jnp.dot(activations, w_value, preferred_element_type=jnp.float32).astype(jnp.bfloat16)
    payload = jnp.concatenate([key_proj, values], axis=1).reshape(
        local_blocks, TILE, 2 * heads_here * HS
    )
    all_valid = jnp.arange(maximum_tiles, dtype=jnp.int32)[None, :] < query_block_counts[:, None]
    owned_ids = device_index * local_blocks + jnp.arange(local_blocks, dtype=jnp.int32)
    wanted = jnp.any(
        (tile_lists[:, :, None] == owned_ids[None, None, :]) & all_valid[:, :, None], axis=1
    )
    wanted = jnp.any(wanted.reshape(seq_devices, local_blocks, local_blocks), axis=1).astype(
        jnp.int32
    )
    slot_ranks = jnp.cumsum(wanted, axis=1) - wanted
    selector = (slot_ranks[:, None, :] == jnp.arange(capacity, dtype=jnp.int32)[None, :, None]) & (
        wanted[:, None, :] > 0
    )
    outgoing = jnp.einsum(
        "dcj,jrf->dcrf", selector.astype(jnp.bfloat16), payload, preferred_element_type=jnp.float32
    ).astype(jnp.bfloat16)
    my_lists = lax.dynamic_slice_in_dim(tile_lists, device_index * local_blocks, local_blocks, 0)
    my_valid = lax.dynamic_slice_in_dim(all_valid, device_index * local_blocks, local_blocks, 0)
    tile_ids = jnp.arange(block_total, dtype=jnp.int32)
    matches = (my_lists[:, :, None] == tile_ids[None, None, :]) & my_valid[:, :, None]
    requested = jnp.any(matches, axis=(0, 1)).astype(jnp.int32).reshape(seq_devices, local_blocks)
    own_ranks = jnp.cumsum(requested, axis=1) - requested
    slot_table = (jnp.arange(seq_devices, dtype=jnp.int32)[:, None] * capacity + own_ranks).reshape(
        -1
    )
    slot_index = jnp.sum(jnp.where(matches, slot_table[None, None, :], 0), axis=2)
    arrived = lax.all_to_all(outgoing, ("seq", "sub"), split_axis=0, concat_axis=0, tiled=True)
    arrived = arrived.reshape(seq_devices * capacity, TILE, 2 * heads_here * HS)
    slot_tiles = jnp.take(arrived, slot_index.reshape(-1), axis=0)
    slot_tiles = slot_tiles.reshape(local_blocks, maximum_tiles, TILE, 2, heads_here, HS)
    key_slots = slot_tiles[:, :, :, 0]
    value_slots = slot_tiles[:, :, :, 1]
    query_blocks = query_rows.reshape(local_blocks, TILE, heads_here, HS)
    scores = jnp.einsum(
        "bihd,bmjhd->hbimj", query_blocks, key_slots, preferred_element_type=jnp.float32
    ) * HS ** (-0.5)
    valid_mask = my_valid[None, :, None, :, None]
    row_max = jnp.max(jnp.where(valid_mask, scores, -1e30), axis=(3, 4), keepdims=True)
    weights = jnp.where(valid_mask, jnp.exp(scores - row_max), 0.0)
    onehot = matches.astype(jnp.float32)
    for round_number in range(BALANCING_ROUNDS):
        weights = weights / jnp.sum(weights, axis=(3, 4), keepdims=True)
        partial_cols = jnp.sum(weights, axis=2)
        column_complete = jnp.einsum(
            "bmt,hbmj->thj", onehot, partial_cols, precision=lax.Precision.HIGHEST
        ).reshape(seq_devices, local_blocks, heads_here, TILE)
        from_all = lax.all_to_all(
            column_complete, ("seq", "sub"), split_axis=0, concat_axis=0, tiled=True
        )
        owned_sums = jnp.sum(from_all, axis=0)
        spread = jnp.broadcast_to(owned_sums[None], (seq_devices,) + owned_sums.shape)
        totals = lax.all_to_all(
            spread, ("seq", "sub"), split_axis=0, concat_axis=0, tiled=True
        ).reshape(block_total, heads_here, TILE)
        per_slot = jnp.einsum("bmt,thj->hbmj", onehot, totals, precision=lax.Precision.HIGHEST)
        weights = weights / jnp.maximum(per_slot[:, :, None, :, :], COLUMN_FLOOR)
    probabilities = weights.astype(jnp.bfloat16)
    attended = jnp.einsum(
        "hbimj,bmjhd->bihd", probabilities, value_slots, preferred_element_type=jnp.float32
    )
    attended = attended.astype(jnp.bfloat16).reshape(row_count, heads_here * HS)
    head_count = lax.axis_size("head")
    if head_count != 2:
        partial_out = jnp.dot(attended, w_out, preferred_element_type=jnp.float32)
        return lax.psum_scatter(
            partial_out.astype(jnp.bfloat16), "head", scatter_dimension=1, tiled=True
        )
    head_index = lax.axis_index("head")
    width = w_out.shape[1] // 2
    other_cols = lax.dynamic_slice_in_dim(w_out, (1 - head_index) * width, width, 1)
    my_cols = lax.dynamic_slice_in_dim(w_out, head_index * width, width, 1)
    other_part = jnp.dot(attended, other_cols, preferred_element_type=jnp.float32)
    received = lax.ppermute(other_part.astype(jnp.bfloat16), "head", perm=[(0, 1), (1, 0)])
    my_part = jnp.dot(attended, my_cols, preferred_element_type=jnp.float32)
    return (my_part + received.astype(jnp.float32)).astype(jnp.bfloat16)


def solution(mesh):
    placed = (
        P(("groups", "seq", "sub"), None),
        P(None, "head"),
        P(None, "head"),
        P(None, "head"),
        P("head", None),
        P("groups", None),
        P("groups"),
    )
    return jax.shard_map(
        body,
        mesh=mesh,
        in_specs=placed,
        out_specs=P(("groups", "seq", "sub"), "head"),
        check_vma=False,
    )
```

```python
import jax
import jax.numpy as jnp
from jax import lax
from jax.sharding import PartitionSpec as P

HS = 128
TILE = 128
BALANCING_ROUNDS = 3


COLUMN_FLOOR = 0.1


def body(activations, w_query, w_key, w_value, w_out, tile_lists, query_block_counts):
    seq_devices = lax.axis_size(("seq", "sub"))
    device_index = lax.axis_index(("seq", "sub"))
    block_total = tile_lists.shape[0]
    maximum_tiles = tile_lists.shape[1]
    row_count = activations.shape[0]
    local_blocks = row_count // TILE
    heads_here = w_query.shape[1] // HS
    capacity = local_blocks * (maximum_tiles // 2) // seq_devices
    head_count = lax.axis_size("head")
    head_index = lax.axis_index("head")
    rows_part = TILE // head_count
    query_rows = jnp.dot(activations, w_query, preferred_element_type=jnp.float32).astype(
        jnp.bfloat16
    )
    act_tiles = activations.reshape(local_blocks, TILE, activations.shape[1])
    my_rows = lax.dynamic_slice_in_dim(act_tiles, head_index * rows_part, rows_part, 1)
    all_valid = jnp.arange(maximum_tiles, dtype=jnp.int32)[None, :] < query_block_counts[:, None]
    owned_ids = device_index * local_blocks + jnp.arange(local_blocks, dtype=jnp.int32)
    wanted = jnp.any(
        (tile_lists[:, :, None] == owned_ids[None, None, :]) & all_valid[:, :, None], axis=1
    )
    wanted = jnp.any(wanted.reshape(seq_devices, local_blocks, local_blocks), axis=1).astype(
        jnp.int32
    )
    slot_ranks = jnp.cumsum(wanted, axis=1) - wanted
    selector = (slot_ranks[:, None, :] == jnp.arange(capacity, dtype=jnp.int32)[None, :, None]) & (
        wanted[:, None, :] > 0
    )
    outgoing = jnp.einsum(
        "dcj,jrf->cdrf", selector.astype(jnp.bfloat16), my_rows, preferred_element_type=jnp.float32
    ).astype(jnp.bfloat16)
    my_lists = lax.dynamic_slice_in_dim(tile_lists, device_index * local_blocks, local_blocks, 0)
    my_valid = lax.dynamic_slice_in_dim(all_valid, device_index * local_blocks, local_blocks, 0)
    tile_ids = jnp.arange(block_total, dtype=jnp.int32)
    matches = (my_lists[:, :, None] == tile_ids[None, None, :]) & my_valid[:, :, None]
    requested = jnp.any(matches, axis=(0, 1)).astype(jnp.int32).reshape(seq_devices, local_blocks)
    own_ranks = jnp.cumsum(requested, axis=1) - requested
    sources = jnp.arange(seq_devices, dtype=jnp.int32)
    if seq_devices & (seq_devices - 1) == 0:
        source_steps = jnp.bitwise_xor(sources, device_index)
    else:
        source_steps = (device_index - sources) % seq_devices
    slot_table = (source_steps[:, None] * capacity + own_ranks).reshape(-1)
    slot_index = jnp.sum(jnp.where(matches, slot_table[None, None, :], 0), axis=2)
    key_weights = w_key.reshape(w_key.shape[0], heads_here, HS)
    value_weights = w_value.reshape(w_value.shape[0], heads_here, HS)
    power_of_two = seq_devices & (seq_devices - 1) == 0
    own_selector = selector[device_index].astype(jnp.bfloat16)
    key_parts = []
    value_parts = []
    for step in range(seq_devices):
        if step == 0:
            if head_count == 2:
                other_rows = lax.dynamic_slice_in_dim(
                    act_tiles, (1 - head_index) * rows_part, rows_part, 1
                )
                full = jnp.concatenate([my_rows, other_rows], axis=1)
            else:
                full = act_tiles
            full = jnp.einsum(
                "cj,jrf->crf", own_selector, full, preferred_element_type=jnp.float32
            ).astype(jnp.bfloat16)
        else:
            if power_of_two:
                target = jnp.bitwise_xor(device_index, step)
                pairs = [(i, i ^ step) for i in range(seq_devices)]
            else:
                target = (device_index + step) % seq_devices
                pairs = [(i, (i + step) % seq_devices) for i in range(seq_devices)]
            piece = lax.dynamic_index_in_dim(outgoing, target, axis=1, keepdims=False)
            got = lax.ppermute(piece, ("seq", "sub"), perm=pairs)
            if head_count == 2:
                partner = lax.ppermute(got, "head", perm=[(0, 1), (1, 0)])
                full = jnp.concatenate([got, partner], axis=1)
            else:
                full = lax.all_gather(got, "head", axis=1, tiled=True)
        key_parts.append(
            jnp.einsum(
                "cjf,fhd->chjd", full, key_weights, preferred_element_type=jnp.float32
            ).astype(jnp.bfloat16)
        )
        value_parts.append(
            jnp.einsum(
                "cjf,fhd->chjd", full, value_weights, preferred_element_type=jnp.float32
            ).astype(jnp.bfloat16)
        )
    key_all = jnp.concatenate(key_parts, axis=0)
    value_all = jnp.concatenate(value_parts, axis=0)
    flat_index = slot_index.reshape(-1)
    key_slots = jnp.take(key_all, flat_index, axis=0, mode="clip").reshape(
        local_blocks, maximum_tiles, heads_here, TILE, HS
    )
    value_slots = jnp.take(value_all, flat_index, axis=0, mode="clip").reshape(
        local_blocks, maximum_tiles, heads_here, TILE, HS
    )
    query_blocks = query_rows.reshape(local_blocks, TILE, heads_here, HS)
    scores = jnp.einsum(
        "bihd,bmhjd->hbimj", query_blocks, key_slots, preferred_element_type=jnp.float32
    ) * HS ** (-0.5)
    valid_mask = my_valid[None, :, None, :, None]
    row_max = jnp.max(jnp.where(valid_mask, scores, -1e30), axis=(3, 4), keepdims=True)
    weights = jnp.where(valid_mask, jnp.exp(scores - row_max), 0.0)
    onehot = matches.astype(jnp.float32)
    for round_number in range(BALANCING_ROUNDS):
        weights = weights / jnp.sum(weights, axis=(3, 4), keepdims=True)
        partial_cols = jnp.sum(weights, axis=2)
        column_complete = jnp.einsum(
            "bmt,hbmj->thj", onehot, partial_cols, precision=lax.Precision.HIGHEST
        ).reshape(seq_devices, local_blocks, heads_here, TILE)
        from_all = lax.all_to_all(
            column_complete, ("seq", "sub"), split_axis=0, concat_axis=0, tiled=True
        )
        owned_sums = jnp.sum(from_all, axis=0)
        spread = jnp.broadcast_to(owned_sums[None], (seq_devices,) + owned_sums.shape)
        totals = lax.all_to_all(
            spread, ("seq", "sub"), split_axis=0, concat_axis=0, tiled=True
        ).reshape(block_total, heads_here, TILE)
        per_slot = jnp.einsum("bmt,thj->hbmj", onehot, totals, precision=lax.Precision.HIGHEST)
        weights = weights / jnp.maximum(per_slot[:, :, None, :, :], COLUMN_FLOOR)
    probabilities = weights.astype(jnp.bfloat16)
    attended = jnp.einsum(
        "hbimj,bmhjd->bihd", probabilities, value_slots, preferred_element_type=jnp.float32
    )
    attended = attended.astype(jnp.bfloat16).reshape(row_count, heads_here * HS)
    head_count = lax.axis_size("head")
    if head_count != 2:
        partial_out = jnp.dot(attended, w_out, preferred_element_type=jnp.float32)
        return lax.psum_scatter(
            partial_out.astype(jnp.bfloat16), "head", scatter_dimension=1, tiled=True
        )
    head_index = lax.axis_index("head")
    width = w_out.shape[1] // 2
    other_cols = lax.dynamic_slice_in_dim(w_out, (1 - head_index) * width, width, 1)
    my_cols = lax.dynamic_slice_in_dim(w_out, head_index * width, width, 1)
    other_part = jnp.dot(attended, other_cols, preferred_element_type=jnp.float32)
    received = lax.ppermute(other_part.astype(jnp.bfloat16), "head", perm=[(0, 1), (1, 0)])
    my_part = jnp.dot(attended, my_cols, preferred_element_type=jnp.float32)
    return (my_part + received.astype(jnp.float32)).astype(jnp.bfloat16)


def solution(mesh):
    placed = (
        P(("groups", "seq", "sub"), None),
        P(None, "head"),
        P(None, "head"),
        P(None, "head"),
        P("head", None),
        P("groups", None),
        P("groups"),
    )
    return jax.shard_map(
        body,
        mesh=mesh,
        in_specs=placed,
        out_specs=P(("groups", "seq", "sub"), "head"),
        check_vma=False,
    )
```

```python
import jax
import jax.numpy as jnp
from jax import lax
from jax.sharding import PartitionSpec as P

HS = 128
TILE = 128
BALANCING_ROUNDS = 3


COLUMN_FLOOR = 0.1


def body(activations, w_query, w_key, w_value, w_out, tile_lists, query_block_counts):
    seq_devices = lax.axis_size(("seq", "sub"))
    device_index = lax.axis_index(("seq", "sub"))
    block_total = tile_lists.shape[0]
    maximum_tiles = tile_lists.shape[1]
    row_count = activations.shape[0]
    local_blocks = row_count // TILE
    heads_here = w_query.shape[1] // HS
    capacity = local_blocks * (maximum_tiles // 2) // seq_devices
    head_count = lax.axis_size("head")
    head_index = lax.axis_index("head")
    rows_part = TILE // head_count
    query_rows = jnp.dot(activations, w_query, preferred_element_type=jnp.float32).astype(
        jnp.bfloat16
    )
    act_tiles = activations.reshape(local_blocks, TILE, activations.shape[1])
    my_rows = lax.dynamic_slice_in_dim(act_tiles, head_index * rows_part, rows_part, 1)
    all_valid = jnp.arange(maximum_tiles, dtype=jnp.int32)[None, :] < query_block_counts[:, None]
    owned_ids = device_index * local_blocks + jnp.arange(local_blocks, dtype=jnp.int32)
    wanted = jnp.any(
        (tile_lists[:, :, None] == owned_ids[None, None, :]) & all_valid[:, :, None], axis=1
    )
    wanted = jnp.any(wanted.reshape(seq_devices, local_blocks, local_blocks), axis=1).astype(
        jnp.int32
    )
    slot_ranks = jnp.cumsum(wanted, axis=1) - wanted
    selector = (slot_ranks[:, None, :] == jnp.arange(capacity, dtype=jnp.int32)[None, :, None]) & (
        wanted[:, None, :] > 0
    )
    send_index = jnp.sum(
        selector.astype(jnp.int32) * jnp.arange(local_blocks, dtype=jnp.int32)[None, None, :], axis=2
    )
    my_lists = lax.dynamic_slice_in_dim(tile_lists, device_index * local_blocks, local_blocks, 0)
    my_valid = lax.dynamic_slice_in_dim(all_valid, device_index * local_blocks, local_blocks, 0)
    tile_ids = jnp.arange(block_total, dtype=jnp.int32)
    matches = (my_lists[:, :, None] == tile_ids[None, None, :]) & my_valid[:, :, None]
    requested = jnp.any(matches, axis=(0, 1)).astype(jnp.int32).reshape(seq_devices, local_blocks)
    own_ranks = jnp.cumsum(requested, axis=1) - requested
    sources = jnp.arange(seq_devices, dtype=jnp.int32)
    if seq_devices & (seq_devices - 1) == 0:
        source_steps = jnp.bitwise_xor(sources, device_index)
    else:
        source_steps = (device_index - sources) % seq_devices
    slot_table = (source_steps[:, None] * capacity + own_ranks).reshape(-1)
    slot_index = jnp.sum(jnp.where(matches, slot_table[None, None, :], 0), axis=2)
    key_weights = w_key.reshape(w_key.shape[0], heads_here, HS)
    value_weights = w_value.reshape(w_value.shape[0], heads_here, HS)
    power_of_two = seq_devices & (seq_devices - 1) == 0
    own_index = send_index[device_index]
    key_parts = {}
    value_parts = {}
    for step in sorted(range(seq_devices), key=lambda k: (k != 0, -k)):
        if step == 0:
            if head_count == 2:
                other_rows = lax.dynamic_slice_in_dim(
                    act_tiles, (1 - head_index) * rows_part, rows_part, 1
                )
                full = jnp.concatenate([my_rows, other_rows], axis=1)
            else:
                full = act_tiles
            full = jnp.take(full, own_index, axis=0, mode="clip")
        else:
            if power_of_two:
                target = jnp.bitwise_xor(device_index, step)
                pairs = [(i, i ^ step) for i in range(seq_devices)]
            else:
                target = (device_index + step) % seq_devices
                pairs = [(i, (i + step) % seq_devices) for i in range(seq_devices)]
            piece = jnp.take(my_rows, send_index[target], axis=0, mode="clip")
            got = lax.ppermute(piece, ("seq", "sub"), perm=pairs)
            if head_count == 2:
                partner = lax.ppermute(got, "head", perm=[(0, 1), (1, 0)])
                full = jnp.concatenate([got, partner], axis=1)
            else:
                full = lax.all_gather(got, "head", axis=1, tiled=True)
        key_parts[step] = jnp.einsum(
            "cjf,fhd->chjd", full, key_weights, preferred_element_type=jnp.float32
        ).astype(jnp.bfloat16)
        value_parts[step] = jnp.einsum(
            "cjf,fhd->chjd", full, value_weights, preferred_element_type=jnp.float32
        ).astype(jnp.bfloat16)
    key_all = jnp.concatenate([key_parts[k] for k in range(seq_devices)], axis=0)
    value_all = jnp.concatenate([value_parts[k] for k in range(seq_devices)], axis=0)
    flat_index = slot_index.reshape(-1)
    key_slots = jnp.take(key_all, flat_index, axis=0, mode="clip").reshape(
        local_blocks, maximum_tiles, heads_here, TILE, HS
    )
    value_slots = jnp.take(value_all, flat_index, axis=0, mode="clip").reshape(
        local_blocks, maximum_tiles, heads_here, TILE, HS
    )
    query_blocks = query_rows.reshape(local_blocks, TILE, heads_here, HS)
    scores = jnp.einsum(
        "bihd,bmhjd->hbimj", query_blocks, key_slots, preferred_element_type=jnp.float32
    ) * HS ** (-0.5)
    valid_mask = my_valid[None, :, None, :, None]
    row_max = jnp.max(jnp.where(valid_mask, scores, -1e30), axis=(3, 4), keepdims=True)
    weights = jnp.where(valid_mask, jnp.exp(scores - row_max), 0.0)
    onehot = matches.astype(jnp.float32)
    for round_number in range(BALANCING_ROUNDS):
        weights = weights / jnp.sum(weights, axis=(3, 4), keepdims=True)
        partial_cols = jnp.sum(weights, axis=2)
        column_complete = jnp.einsum(
            "bmt,hbmj->thj", onehot, partial_cols, precision=lax.Precision.HIGHEST
        ).reshape(seq_devices, local_blocks, heads_here, TILE)
        from_all = lax.all_to_all(
            column_complete, ("seq", "sub"), split_axis=0, concat_axis=0, tiled=True
        )
        owned_sums = jnp.sum(from_all, axis=0)
        spread = jnp.broadcast_to(owned_sums[None], (seq_devices,) + owned_sums.shape)
        totals = lax.all_to_all(
            spread, ("seq", "sub"), split_axis=0, concat_axis=0, tiled=True
        ).reshape(block_total, heads_here, TILE)
        per_slot = jnp.einsum("bmt,thj->hbmj", onehot, totals, precision=lax.Precision.HIGHEST)
        weights = weights / jnp.maximum(per_slot[:, :, None, :, :], COLUMN_FLOOR)
    probabilities = weights.astype(jnp.bfloat16)
    attended = jnp.einsum(
        "hbimj,bmhjd->bihd", probabilities, value_slots, preferred_element_type=jnp.float32
    )
    attended = attended.astype(jnp.bfloat16).reshape(row_count, heads_here * HS)
    head_count = lax.axis_size("head")
    if head_count != 2:
        partial_out = jnp.dot(attended, w_out, preferred_element_type=jnp.float32)
        return lax.psum_scatter(
            partial_out.astype(jnp.bfloat16), "head", scatter_dimension=1, tiled=True
        )
    head_index = lax.axis_index("head")
    width = w_out.shape[1] // 2
    other_cols = lax.dynamic_slice_in_dim(w_out, (1 - head_index) * width, width, 1)
    my_cols = lax.dynamic_slice_in_dim(w_out, head_index * width, width, 1)
    other_part = jnp.dot(attended, other_cols, preferred_element_type=jnp.float32)
    received = lax.ppermute(other_part.astype(jnp.bfloat16), "head", perm=[(0, 1), (1, 0)])
    my_part = jnp.dot(attended, my_cols, preferred_element_type=jnp.float32)
    return (my_part + received.astype(jnp.float32)).astype(jnp.bfloat16)


def solution(mesh):
    placed = (
        P(("groups", "seq", "sub"), None),
        P(None, "head"),
        P(None, "head"),
        P(None, "head"),
        P("head", None),
        P("groups", None),
        P("groups"),
    )
    return jax.shard_map(
        body,
        mesh=mesh,
        in_specs=placed,
        out_specs=P(("groups", "seq", "sub"), "head"),
        check_vma=False,
    )
```

```python
import jax
import jax.numpy as jnp
from jax import lax
from jax.sharding import PartitionSpec as P

HS = 128
TILE = 128
BALANCING_ROUNDS = 3


COLUMN_FLOOR = 0.1


def body(activations, w_query, w_key, w_value, w_out, tile_lists, query_block_counts):
    seq_devices = lax.axis_size(("seq", "sub"))
    device_index = lax.axis_index(("seq", "sub"))
    block_total = tile_lists.shape[0]
    maximum_tiles = tile_lists.shape[1]
    row_count = activations.shape[0]
    local_blocks = row_count // TILE
    heads_here = w_query.shape[1] // HS
    capacity = local_blocks * (maximum_tiles // 2) // seq_devices
    head_count = lax.axis_size("head")
    head_index = lax.axis_index("head")
    rows_part = TILE // head_count
    query_rows = jnp.dot(activations, w_query, preferred_element_type=jnp.float32).astype(
        jnp.bfloat16
    )
    act_tiles = activations.reshape(local_blocks, TILE, activations.shape[1])
    my_rows = lax.dynamic_slice_in_dim(act_tiles, head_index * rows_part, rows_part, 1)
    all_valid = jnp.arange(maximum_tiles, dtype=jnp.int32)[None, :] < query_block_counts[:, None]
    owned_ids = device_index * local_blocks + jnp.arange(local_blocks, dtype=jnp.int32)
    wanted = jnp.any(
        (tile_lists[:, :, None] == owned_ids[None, None, :]) & all_valid[:, :, None], axis=1
    )
    wanted = jnp.any(wanted.reshape(seq_devices, local_blocks, local_blocks), axis=1).astype(
        jnp.int32
    )
    slot_ranks = jnp.cumsum(wanted, axis=1) - wanted
    selector = (slot_ranks[:, None, :] == jnp.arange(capacity, dtype=jnp.int32)[None, :, None]) & (
        wanted[:, None, :] > 0
    )
    send_index = jnp.sum(
        selector.astype(jnp.int32) * jnp.arange(local_blocks, dtype=jnp.int32)[None, None, :], axis=2
    )
    my_lists = lax.dynamic_slice_in_dim(tile_lists, device_index * local_blocks, local_blocks, 0)
    my_valid = lax.dynamic_slice_in_dim(all_valid, device_index * local_blocks, local_blocks, 0)
    tile_ids = jnp.arange(block_total, dtype=jnp.int32)
    matches = (my_lists[:, :, None] == tile_ids[None, None, :]) & my_valid[:, :, None]
    requested = jnp.any(matches, axis=(0, 1)).astype(jnp.int32).reshape(seq_devices, local_blocks)
    own_ranks = jnp.cumsum(requested, axis=1) - requested
    sources = jnp.arange(seq_devices, dtype=jnp.int32)
    if seq_devices & (seq_devices - 1) == 0:
        source_steps = jnp.bitwise_xor(sources, device_index)
    else:
        source_steps = (device_index - sources) % seq_devices
    slot_table = (source_steps[:, None] * capacity + own_ranks).reshape(-1)
    slot_index = jnp.sum(jnp.where(matches, slot_table[None, None, :], 0), axis=2)
    key_weights = w_key.reshape(w_key.shape[0], heads_here, HS)
    value_weights = w_value.reshape(w_value.shape[0], heads_here, HS)
    power_of_two = seq_devices & (seq_devices - 1) == 0
    own_index = send_index[device_index]
    key_parts = {}
    value_parts = {}
    previous_far = None
    for step in sorted(range(seq_devices), key=lambda k: (k != 0, -k)):
        if step == 0:
            if head_count == 2:
                other_rows = lax.dynamic_slice_in_dim(
                    act_tiles, (1 - head_index) * rows_part, rows_part, 1
                )
                full = jnp.concatenate([my_rows, other_rows], axis=1)
            else:
                full = act_tiles
            full = jnp.take(full, own_index, axis=0, mode="clip")
        else:
            if power_of_two:
                target = jnp.bitwise_xor(device_index, step)
                pairs = [(i, i ^ step) for i in range(seq_devices)]
            else:
                target = (device_index + step) % seq_devices
                pairs = [(i, (i + step) % seq_devices) for i in range(seq_devices)]
            piece = jnp.take(my_rows, send_index[target], axis=0, mode="clip")
            if step >= seq_devices // 2 and previous_far is not None:
                piece, _ = lax.optimization_barrier((piece, previous_far))
            got = lax.ppermute(piece, ("seq", "sub"), perm=pairs)
            if step >= seq_devices // 2:
                previous_far = got
            if head_count == 2:
                partner = lax.ppermute(got, "head", perm=[(0, 1), (1, 0)])
                full = jnp.concatenate([got, partner], axis=1)
            else:
                full = lax.all_gather(got, "head", axis=1, tiled=True)
        key_parts[step] = jnp.einsum(
            "cjf,fhd->chjd", full, key_weights, preferred_element_type=jnp.float32
        ).astype(jnp.bfloat16)
        value_parts[step] = jnp.einsum(
            "cjf,fhd->chjd", full, value_weights, preferred_element_type=jnp.float32
        ).astype(jnp.bfloat16)
    key_all = jnp.concatenate([key_parts[k] for k in range(seq_devices)], axis=0)
    value_all = jnp.concatenate([value_parts[k] for k in range(seq_devices)], axis=0)
    flat_index = slot_index.reshape(-1)
    key_slots = jnp.take(key_all, flat_index, axis=0, mode="clip").reshape(
        local_blocks, maximum_tiles, heads_here, TILE, HS
    )
    value_slots = jnp.take(value_all, flat_index, axis=0, mode="clip").reshape(
        local_blocks, maximum_tiles, heads_here, TILE, HS
    )
    query_blocks = query_rows.reshape(local_blocks, TILE, heads_here, HS)
    scores = jnp.einsum(
        "bihd,bmhjd->hbimj", query_blocks, key_slots, preferred_element_type=jnp.float32
    ) * HS ** (-0.5)
    valid_mask = my_valid[None, :, None, :, None]
    row_max = jnp.max(jnp.where(valid_mask, scores, -1e30), axis=(3, 4), keepdims=True)
    weights = jnp.where(valid_mask, jnp.exp(scores - row_max), 0.0)
    onehot = matches.astype(jnp.float32)
    for round_number in range(BALANCING_ROUNDS):
        weights = weights / jnp.sum(weights, axis=(3, 4), keepdims=True)
        partial_cols = jnp.sum(weights, axis=2)
        column_complete = jnp.einsum(
            "bmt,hbmj->thj", onehot, partial_cols, precision=lax.Precision.HIGHEST
        ).reshape(seq_devices, local_blocks, heads_here, TILE)
        from_all = lax.all_to_all(
            column_complete, ("seq", "sub"), split_axis=0, concat_axis=0, tiled=True
        )
        owned_sums = jnp.sum(from_all, axis=0)
        spread = jnp.broadcast_to(owned_sums[None], (seq_devices,) + owned_sums.shape)
        totals = lax.all_to_all(
            spread, ("seq", "sub"), split_axis=0, concat_axis=0, tiled=True
        ).reshape(block_total, heads_here, TILE)
        per_slot = jnp.einsum("bmt,thj->hbmj", onehot, totals, precision=lax.Precision.HIGHEST)
        weights = weights / jnp.maximum(per_slot[:, :, None, :, :], COLUMN_FLOOR)
    probabilities = weights.astype(jnp.bfloat16)
    attended = jnp.einsum(
        "hbimj,bmhjd->bihd", probabilities, value_slots, preferred_element_type=jnp.float32
    )
    attended = attended.astype(jnp.bfloat16).reshape(row_count, heads_here * HS)
    head_count = lax.axis_size("head")
    if head_count != 2:
        partial_out = jnp.dot(attended, w_out, preferred_element_type=jnp.float32)
        return lax.psum_scatter(
            partial_out.astype(jnp.bfloat16), "head", scatter_dimension=1, tiled=True
        )
    head_index = lax.axis_index("head")
    width = w_out.shape[1] // 2
    other_cols = lax.dynamic_slice_in_dim(w_out, (1 - head_index) * width, width, 1)
    my_cols = lax.dynamic_slice_in_dim(w_out, head_index * width, width, 1)
    other_part = jnp.dot(attended, other_cols, preferred_element_type=jnp.float32)
    received = lax.ppermute(other_part.astype(jnp.bfloat16), "head", perm=[(0, 1), (1, 0)])
    my_part = jnp.dot(attended, my_cols, preferred_element_type=jnp.float32)
    return (my_part + received.astype(jnp.float32)).astype(jnp.bfloat16)


def solution(mesh):
    placed = (
        P(("groups", "seq", "sub"), None),
        P(None, "head"),
        P(None, "head"),
        P(None, "head"),
        P("head", None),
        P("groups", None),
        P("groups"),
    )
    return jax.shard_map(
        body,
        mesh=mesh,
        in_specs=placed,
        out_specs=P(("groups", "seq", "sub"), "head"),
        check_vma=False,
    )
```

```python
import jax
import jax.numpy as jnp
from jax import lax
from jax.sharding import PartitionSpec as P

HS = 128
TILE = 128
BALANCING_ROUNDS = 3


COLUMN_FLOOR = 0.1


def body(activations, w_query, w_key, w_value, w_out, tile_lists, query_block_counts):
    seq_devices = lax.axis_size(("seq", "sub"))
    device_index = lax.axis_index(("seq", "sub"))
    block_total = tile_lists.shape[0]
    maximum_tiles = tile_lists.shape[1]
    row_count = activations.shape[0]
    local_blocks = row_count // TILE
    heads_here = w_query.shape[1] // HS
    capacity = local_blocks * (maximum_tiles // 2) // seq_devices
    head_count = lax.axis_size("head")
    head_index = lax.axis_index("head")
    rows_part = TILE // head_count
    query_rows = jnp.dot(activations, w_query, preferred_element_type=jnp.float32).astype(
        jnp.bfloat16
    )
    act_tiles = activations.reshape(local_blocks, TILE, activations.shape[1])
    my_rows = lax.dynamic_slice_in_dim(act_tiles, head_index * rows_part, rows_part, 1)
    all_valid = jnp.arange(maximum_tiles, dtype=jnp.int32)[None, :] < query_block_counts[:, None]
    owned_ids = device_index * local_blocks + jnp.arange(local_blocks, dtype=jnp.int32)
    wanted = jnp.any(
        (tile_lists[:, :, None] == owned_ids[None, None, :]) & all_valid[:, :, None], axis=1
    )
    wanted = jnp.any(wanted.reshape(seq_devices, local_blocks, local_blocks), axis=1).astype(
        jnp.int32
    )
    slot_ranks = jnp.cumsum(wanted, axis=1) - wanted
    selector = (slot_ranks[:, None, :] == jnp.arange(capacity, dtype=jnp.int32)[None, :, None]) & (
        wanted[:, None, :] > 0
    )
    send_index = jnp.sum(
        selector.astype(jnp.int32) * jnp.arange(local_blocks, dtype=jnp.int32)[None, None, :], axis=2
    )
    my_lists = lax.dynamic_slice_in_dim(tile_lists, device_index * local_blocks, local_blocks, 0)
    my_valid = lax.dynamic_slice_in_dim(all_valid, device_index * local_blocks, local_blocks, 0)
    tile_ids = jnp.arange(block_total, dtype=jnp.int32)
    matches = (my_lists[:, :, None] == tile_ids[None, None, :]) & my_valid[:, :, None]
    requested = jnp.any(matches, axis=(0, 1)).astype(jnp.int32).reshape(seq_devices, local_blocks)
    own_ranks = jnp.cumsum(requested, axis=1) - requested
    sources = jnp.arange(seq_devices, dtype=jnp.int32)
    if seq_devices & (seq_devices - 1) == 0:
        source_steps = jnp.bitwise_xor(sources, device_index)
    else:
        source_steps = (device_index - sources) % seq_devices
    slot_table = (source_steps[:, None] * capacity + own_ranks).reshape(-1)
    slot_index = jnp.sum(jnp.where(matches, slot_table[None, None, :], 0), axis=2)
    key_weights = w_key.reshape(w_key.shape[0], heads_here, HS)
    value_weights = w_value.reshape(w_value.shape[0], heads_here, HS)
    power_of_two = seq_devices & (seq_devices - 1) == 0
    own_index = send_index[device_index]
    key_parts = {}
    value_parts = {}
    for step in sorted(range(seq_devices), key=lambda k: (k != 0, -k)):
        if step == 0:
            if head_count == 2:
                other_rows = lax.dynamic_slice_in_dim(
                    act_tiles, (1 - head_index) * rows_part, rows_part, 1
                )
                full = jnp.concatenate([my_rows, other_rows], axis=1)
            else:
                full = act_tiles
            full = jnp.take(full, own_index, axis=0, mode="clip")
        else:
            if power_of_two:
                target = jnp.bitwise_xor(device_index, step)
                pairs = [(i, i ^ step) for i in range(seq_devices)]
            else:
                target = (device_index + step) % seq_devices
                pairs = [(i, (i + step) % seq_devices) for i in range(seq_devices)]
            piece = jnp.take(my_rows, send_index[target], axis=0, mode="clip")
            got = lax.ppermute(piece, ("seq", "sub"), perm=pairs)
            if head_count == 2:
                partner = lax.ppermute(got, "head", perm=[(0, 1), (1, 0)])
                full = jnp.concatenate([got, partner], axis=1)
            else:
                full = lax.all_gather(got, "head", axis=1, tiled=True)
        key_parts[step] = jnp.einsum(
            "cjf,fhd->chjd", full, key_weights, preferred_element_type=jnp.float32
        ).astype(jnp.bfloat16)
        value_parts[step] = jnp.einsum(
            "cjf,fhd->chjd", full, value_weights, preferred_element_type=jnp.float32
        ).astype(jnp.bfloat16)
    key_all = jnp.concatenate([key_parts[k] for k in range(seq_devices)], axis=0)
    value_all = jnp.concatenate([value_parts[k] for k in range(seq_devices)], axis=0)
    flat_index = slot_index.reshape(-1)
    key_slots = jnp.take(key_all, flat_index, axis=0, mode="clip").reshape(
        local_blocks, maximum_tiles, heads_here, TILE, HS
    )
    value_slots = jnp.take(value_all, flat_index, axis=0, mode="clip").reshape(
        local_blocks, maximum_tiles, heads_here, TILE, HS
    )
    query_blocks = query_rows.reshape(local_blocks, TILE, heads_here, HS)
    scores = jnp.einsum(
        "bihd,bmhjd->hbimj", query_blocks, key_slots, preferred_element_type=jnp.float32
    ) * HS ** (-0.5)
    valid_mask = my_valid[None, :, None, :, None]
    row_max = jnp.max(jnp.where(valid_mask, scores, -1e30), axis=(3, 4), keepdims=True)
    weights = jnp.where(valid_mask, jnp.exp(scores - row_max), 0.0)
    column_scale = jnp.ones(weights.shape[:2] + weights.shape[3:], jnp.float32)
    onehot = matches.astype(jnp.float32)
    for round_number in range(BALANCING_ROUNDS):
        row_scale = 1.0 / jnp.sum(weights * column_scale[:, :, None], axis=(3, 4))
        partial_cols = column_scale * jnp.sum(weights * row_scale[:, :, :, None, None], axis=2)
        column_complete = jnp.einsum(
            "bmt,hbmj->thj", onehot, partial_cols, precision=lax.Precision.HIGHEST
        ).reshape(seq_devices, local_blocks, heads_here, TILE)
        from_all = lax.all_to_all(
            column_complete, ("seq", "sub"), split_axis=0, concat_axis=0, tiled=True
        )
        owned_sums = jnp.sum(from_all, axis=0)
        spread = jnp.broadcast_to(owned_sums[None], (seq_devices,) + owned_sums.shape)
        totals = lax.all_to_all(
            spread, ("seq", "sub"), split_axis=0, concat_axis=0, tiled=True
        ).reshape(block_total, heads_here, TILE)
        per_slot = jnp.einsum("bmt,thj->hbmj", onehot, totals, precision=lax.Precision.HIGHEST)
        column_scale = column_scale / jnp.maximum(per_slot, COLUMN_FLOOR)
    probabilities = (
        weights * row_scale[:, :, :, None, None] * column_scale[:, :, None]
    ).astype(jnp.bfloat16)
    attended = jnp.einsum(
        "hbimj,bmhjd->bihd", probabilities, value_slots, preferred_element_type=jnp.float32
    )
    attended = attended.astype(jnp.bfloat16).reshape(row_count, heads_here * HS)
    head_count = lax.axis_size("head")
    if head_count != 2:
        partial_out = jnp.dot(attended, w_out, preferred_element_type=jnp.float32)
        return lax.psum_scatter(
            partial_out.astype(jnp.bfloat16), "head", scatter_dimension=1, tiled=True
        )
    head_index = lax.axis_index("head")
    width = w_out.shape[1] // 2
    other_cols = lax.dynamic_slice_in_dim(w_out, (1 - head_index) * width, width, 1)
    my_cols = lax.dynamic_slice_in_dim(w_out, head_index * width, width, 1)
    other_part = jnp.dot(attended, other_cols, preferred_element_type=jnp.float32)
    received = lax.ppermute(other_part.astype(jnp.bfloat16), "head", perm=[(0, 1), (1, 0)])
    my_part = jnp.dot(attended, my_cols, preferred_element_type=jnp.float32)
    return (my_part + received.astype(jnp.float32)).astype(jnp.bfloat16)


def solution(mesh):
    placed = (
        P(("groups", "seq", "sub"), None),
        P(None, "head"),
        P(None, "head"),
        P(None, "head"),
        P("head", None),
        P("groups", None),
        P("groups"),
    )
    return jax.shard_map(
        body,
        mesh=mesh,
        in_specs=placed,
        out_specs=P(("groups", "seq", "sub"), "head"),
        check_vma=False,
    )
```

```python
import jax
import jax.numpy as jnp
from jax import lax
from jax.sharding import PartitionSpec as P

HS = 128
TILE = 128
BALANCING_ROUNDS = 3


COLUMN_FLOOR = 0.1


def body(activations, w_query, w_key, w_value, w_out, tile_lists, query_block_counts):
    seq_devices = lax.axis_size(("seq", "sub"))
    device_index = lax.axis_index(("seq", "sub"))
    block_total = tile_lists.shape[0]
    maximum_tiles = tile_lists.shape[1]
    row_count = activations.shape[0]
    local_blocks = row_count // TILE
    heads_here = w_query.shape[1] // HS
    capacity = local_blocks * (maximum_tiles // 2) // seq_devices
    head_count = lax.axis_size("head")
    head_index = lax.axis_index("head")
    rows_part = TILE // head_count
    query_rows = jnp.dot(activations, w_query, preferred_element_type=jnp.float32).astype(
        jnp.bfloat16
    )
    act_tiles = activations.reshape(local_blocks, TILE, activations.shape[1])
    my_rows = lax.dynamic_slice_in_dim(act_tiles, head_index * rows_part, rows_part, 1)
    all_valid = jnp.arange(maximum_tiles, dtype=jnp.int32)[None, :] < query_block_counts[:, None]
    owned_ids = device_index * local_blocks + jnp.arange(local_blocks, dtype=jnp.int32)
    wanted = jnp.any(
        (tile_lists[:, :, None] == owned_ids[None, None, :]) & all_valid[:, :, None], axis=1
    )
    wanted = jnp.any(wanted.reshape(seq_devices, local_blocks, local_blocks), axis=1).astype(
        jnp.int32
    )
    slot_ranks = jnp.cumsum(wanted, axis=1) - wanted
    selector = (slot_ranks[:, None, :] == jnp.arange(capacity, dtype=jnp.int32)[None, :, None]) & (
        wanted[:, None, :] > 0
    )
    send_index = jnp.sum(
        selector.astype(jnp.int32) * jnp.arange(local_blocks, dtype=jnp.int32)[None, None, :], axis=2
    )
    my_lists = lax.dynamic_slice_in_dim(tile_lists, device_index * local_blocks, local_blocks, 0)
    my_valid = lax.dynamic_slice_in_dim(all_valid, device_index * local_blocks, local_blocks, 0)
    tile_ids = jnp.arange(block_total, dtype=jnp.int32)
    matches = (my_lists[:, :, None] == tile_ids[None, None, :]) & my_valid[:, :, None]
    requested = jnp.any(matches, axis=(0, 1)).astype(jnp.int32).reshape(seq_devices, local_blocks)
    own_ranks = jnp.cumsum(requested, axis=1) - requested
    sources = jnp.arange(seq_devices, dtype=jnp.int32)
    if seq_devices & (seq_devices - 1) == 0:
        source_steps = jnp.bitwise_xor(sources, device_index)
    else:
        source_steps = (device_index - sources) % seq_devices
    slot_table = (source_steps[:, None] * capacity + own_ranks).reshape(-1)
    slot_index = jnp.sum(jnp.where(matches, slot_table[None, None, :], 0), axis=2)
    key_weights = w_key.reshape(w_key.shape[0], heads_here, HS)
    value_weights = w_value.reshape(w_value.shape[0], heads_here, HS)
    power_of_two = seq_devices & (seq_devices - 1) == 0
    own_index = send_index[device_index]
    key_parts = {}
    value_parts = {}
    for step in sorted(range(seq_devices), key=lambda k: (k != 0, -k)):
        if step == 0:
            if head_count == 2:
                other_rows = lax.dynamic_slice_in_dim(
                    act_tiles, (1 - head_index) * rows_part, rows_part, 1
                )
                full = jnp.concatenate([my_rows, other_rows], axis=1)
            else:
                full = act_tiles
            full = jnp.take(full, own_index, axis=0, mode="clip")
        else:
            if power_of_two:
                target = jnp.bitwise_xor(device_index, step)
                pairs = [(i, i ^ step) for i in range(seq_devices)]
            else:
                target = (device_index + step) % seq_devices
                pairs = [(i, (i + step) % seq_devices) for i in range(seq_devices)]
            piece = jnp.take(my_rows, send_index[target], axis=0, mode="clip")
            got = lax.ppermute(piece, ("seq", "sub"), perm=pairs)
            if head_count == 2:
                partner = lax.ppermute(got, "head", perm=[(0, 1), (1, 0)])
                full = jnp.concatenate([got, partner], axis=1)
            else:
                full = lax.all_gather(got, "head", axis=1, tiled=True)
        key_parts[step] = jnp.einsum(
            "cjf,fhd->chjd", full, key_weights, preferred_element_type=jnp.float32
        ).astype(jnp.bfloat16)
        value_parts[step] = jnp.einsum(
            "cjf,fhd->chjd", full, value_weights, preferred_element_type=jnp.float32
        ).astype(jnp.bfloat16)
    key_all = jnp.concatenate([key_parts[k] for k in range(seq_devices)], axis=0)
    value_all = jnp.concatenate([value_parts[k] for k in range(seq_devices)], axis=0)
    flat_index = slot_index.reshape(-1)
    key_slots = jnp.take(key_all, flat_index, axis=0, mode="clip").reshape(
        local_blocks, maximum_tiles, heads_here, TILE, HS
    )
    value_slots = jnp.take(value_all, flat_index, axis=0, mode="clip").reshape(
        local_blocks, maximum_tiles, heads_here, TILE, HS
    )
    query_blocks = query_rows.reshape(local_blocks, TILE, heads_here, HS)
    scores = jnp.einsum(
        "bihd,bmhjd->hbimj", query_blocks, key_slots, preferred_element_type=jnp.float32
    ) * HS ** (-0.5)
    valid_mask = my_valid[None, :, None, :, None]
    row_max = jnp.max(jnp.where(valid_mask, scores, -1e30), axis=(3, 4), keepdims=True)
    weights = jnp.where(valid_mask, jnp.exp(scores - row_max), 0.0)
    column_scale = jnp.ones(weights.shape[:2] + weights.shape[3:], jnp.float32)
    onehot = matches.astype(jnp.float32)
    for round_number in range(BALANCING_ROUNDS):
        row_scale = 1.0 / jnp.sum(weights * column_scale[:, :, None], axis=(3, 4))
        partial_cols = column_scale * jnp.sum(weights * row_scale[:, :, :, None, None], axis=2)
        column_complete = jnp.einsum(
            "bmt,hbmj->thj", onehot, partial_cols, precision=lax.Precision.HIGHEST
        ).reshape(seq_devices, local_blocks, heads_here, TILE)
        from_all = lax.all_to_all(
            column_complete, ("seq", "sub"), split_axis=0, concat_axis=0, tiled=True
        )
        owned_sums = jnp.sum(from_all, axis=0)
        spread = jnp.broadcast_to(owned_sums[None], (seq_devices,) + owned_sums.shape)
        totals = lax.all_to_all(
            spread, ("seq", "sub"), split_axis=0, concat_axis=0, tiled=True
        ).reshape(block_total, heads_here, TILE)
        per_slot = jnp.einsum("bmt,thj->hbmj", onehot, totals, precision=lax.Precision.HIGHEST)
        column_scale = column_scale / jnp.maximum(per_slot, COLUMN_FLOOR)
    probabilities = (
        weights * row_scale[:, :, :, None, None] * column_scale[:, :, None]
    ).astype(jnp.bfloat16)
    head_count = lax.axis_size("head")
    if head_count != 2:
        attended = jnp.einsum(
            "hbimj,bmhjd->bihd", probabilities, value_slots, preferred_element_type=jnp.float32
        )
        attended = attended.astype(jnp.bfloat16).reshape(row_count, heads_here * HS)
        partial_out = jnp.dot(attended, w_out, preferred_element_type=jnp.float32)
        return lax.psum_scatter(
            partial_out.astype(jnp.bfloat16), "head", scatter_dimension=1, tiled=True
        )
    head_index = lax.axis_index("head")
    width = w_out.shape[1] // 2
    other_cols = lax.dynamic_slice_in_dim(w_out, (1 - head_index) * width, width, 1)
    my_cols = lax.dynamic_slice_in_dim(w_out, head_index * width, width, 1)
    pieces = 2 if local_blocks % 2 == 0 else 1
    piece_blocks = local_blocks // pieces
    outputs = []
    for piece_number in range(pieces):
        block_range = slice(piece_number * piece_blocks, (piece_number + 1) * piece_blocks)
        attended = jnp.einsum(
            "hbimj,bmhjd->bihd",
            probabilities[:, block_range],
            value_slots[block_range],
            preferred_element_type=jnp.float32,
        )
        attended = attended.astype(jnp.bfloat16).reshape(piece_blocks * TILE, heads_here * HS)
        other_part = jnp.dot(attended, other_cols, preferred_element_type=jnp.float32)
        received = lax.ppermute(other_part.astype(jnp.bfloat16), "head", perm=[(0, 1), (1, 0)])
        my_part = jnp.dot(attended, my_cols, preferred_element_type=jnp.float32)
        outputs.append((my_part + received.astype(jnp.float32)).astype(jnp.bfloat16))
    return jnp.concatenate(outputs, axis=0)


def solution(mesh):
    placed = (
        P(("groups", "seq", "sub"), None),
        P(None, "head"),
        P(None, "head"),
        P(None, "head"),
        P("head", None),
        P("groups", None),
        P("groups"),
    )
    return jax.shard_map(
        body,
        mesh=mesh,
        in_specs=placed,
        out_specs=P(("groups", "seq", "sub"), "head"),
        check_vma=False,
    )
```

```python
import jax
import jax.numpy as jnp
from jax import lax
from jax.sharding import PartitionSpec as P

HS = 128
TILE = 128
BALANCING_ROUNDS = 3


COLUMN_FLOOR = 0.1


def body(activations, w_query, w_key, w_value, w_out, tile_lists, query_block_counts):
    seq_devices = lax.axis_size(("seq", "sub"))
    device_index = lax.axis_index(("seq", "sub"))
    block_total = tile_lists.shape[0]
    maximum_tiles = tile_lists.shape[1]
    row_count = activations.shape[0]
    local_blocks = row_count // TILE
    heads_here = w_query.shape[1] // HS
    capacity = local_blocks * (maximum_tiles // 2) // seq_devices
    head_count = lax.axis_size("head")
    head_index = lax.axis_index("head")
    rows_part = TILE // head_count
    query_rows = jnp.dot(activations, w_query, preferred_element_type=jnp.float32).astype(
        jnp.bfloat16
    )
    act_tiles = activations.reshape(local_blocks, TILE, activations.shape[1])
    my_rows = lax.dynamic_slice_in_dim(act_tiles, head_index * rows_part, rows_part, 1)
    all_valid = jnp.arange(maximum_tiles, dtype=jnp.int32)[None, :] < query_block_counts[:, None]
    owned_ids = device_index * local_blocks + jnp.arange(local_blocks, dtype=jnp.int32)
    wanted = jnp.any(
        (tile_lists[:, :, None] == owned_ids[None, None, :]) & all_valid[:, :, None], axis=1
    )
    wanted = jnp.any(wanted.reshape(seq_devices, local_blocks, local_blocks), axis=1).astype(
        jnp.int32
    )
    slot_ranks = jnp.cumsum(wanted, axis=1) - wanted
    selector = (slot_ranks[:, None, :] == jnp.arange(capacity, dtype=jnp.int32)[None, :, None]) & (
        wanted[:, None, :] > 0
    )
    send_index = jnp.sum(
        selector.astype(jnp.int32) * jnp.arange(local_blocks, dtype=jnp.int32)[None, None, :], axis=2
    )
    my_lists = lax.dynamic_slice_in_dim(tile_lists, device_index * local_blocks, local_blocks, 0)
    my_valid = lax.dynamic_slice_in_dim(all_valid, device_index * local_blocks, local_blocks, 0)
    tile_ids = jnp.arange(block_total, dtype=jnp.int32)
    matches = (my_lists[:, :, None] == tile_ids[None, None, :]) & my_valid[:, :, None]
    requested = jnp.any(matches, axis=(0, 1)).astype(jnp.int32).reshape(seq_devices, local_blocks)
    own_ranks = jnp.cumsum(requested, axis=1) - requested
    sources = jnp.arange(seq_devices, dtype=jnp.int32)
    if seq_devices & (seq_devices - 1) == 0:
        source_steps = jnp.bitwise_xor(sources, device_index)
    else:
        source_steps = (device_index - sources) % seq_devices
    slot_table = (source_steps[:, None] * capacity + own_ranks).reshape(-1)
    slot_index = jnp.sum(jnp.where(matches, slot_table[None, None, :], 0), axis=2)
    key_weights = w_key.reshape(w_key.shape[0], heads_here, HS)
    value_weights = w_value.reshape(w_value.shape[0], heads_here, HS)
    power_of_two = seq_devices & (seq_devices - 1) == 0
    own_index = send_index[device_index]
    def project(full):
        keys = jnp.einsum("cjf,fhd->chjd", full, key_weights, preferred_element_type=jnp.float32)
        vals = jnp.einsum("cjf,fhd->chjd", full, value_weights, preferred_element_type=jnp.float32)
        return keys.astype(jnp.bfloat16), vals.astype(jnp.bfloat16)

    def exchange(step, first_tile, last_tile, after):
        if power_of_two:
            target = jnp.bitwise_xor(device_index, step)
            pairs = [(i, i ^ step) for i in range(seq_devices)]
        else:
            target = (device_index + step) % seq_devices
            pairs = [(i, (i + step) % seq_devices) for i in range(seq_devices)]
        chosen = send_index[target][first_tile:last_tile]
        piece = jnp.take(my_rows, chosen, axis=0, mode="clip")
        if after:
            piece, _ = lax.optimization_barrier((piece, after))
        return lax.ppermute(piece, ("seq", "sub"), perm=pairs)

    def widen(got):
        if head_count == 2:
            partner = lax.ppermute(got, "head", perm=[(0, 1), (1, 0)])
            return jnp.concatenate([got, partner], axis=1)
        return lax.all_gather(got, "head", axis=1, tiled=True)

    if head_count == 2:
        other_rows = lax.dynamic_slice_in_dim(act_tiles, (1 - head_index) * rows_part, rows_part, 1)
        own_full = jnp.concatenate([my_rows, other_rows], axis=1)
    else:
        own_full = act_tiles
    key_parts = {}
    value_parts = {}
    key_parts[0], value_parts[0] = project(jnp.take(own_full, own_index, axis=0, mode="clip"))
    far_steps = [k for k in range(1, seq_devices) if k >= seq_devices // 2]
    near_steps = [k for k in range(1, seq_devices) if k < seq_devices // 2]
    split = capacity // 2 if capacity >= 2 else capacity
    early = {k: exchange(k, 0, split, None) for k in reversed(far_steps)}
    late = {}
    if split < capacity:
        held = tuple(early[k] for k in far_steps)
        late = {k: exchange(k, split, capacity, held) for k in reversed(far_steps)}
    for k in near_steps:
        key_parts[k], value_parts[k] = project(widen(exchange(k, 0, capacity, None)))
    for k in far_steps:
        pieces = [project(widen(early[k]))]
        if k in late:
            pieces.append(project(widen(late[k])))
        key_parts[k] = jnp.concatenate([p[0] for p in pieces], axis=0)
        value_parts[k] = jnp.concatenate([p[1] for p in pieces], axis=0)
    key_all = jnp.concatenate([key_parts[k] for k in range(seq_devices)], axis=0)
    value_all = jnp.concatenate([value_parts[k] for k in range(seq_devices)], axis=0)
    flat_index = slot_index.reshape(-1)
    key_slots = jnp.take(key_all, flat_index, axis=0, mode="clip").reshape(
        local_blocks, maximum_tiles, heads_here, TILE, HS
    )
    value_slots = jnp.take(value_all, flat_index, axis=0, mode="clip").reshape(
        local_blocks, maximum_tiles, heads_here, TILE, HS
    )
    query_blocks = query_rows.reshape(local_blocks, TILE, heads_here, HS)
    scores = jnp.einsum(
        "bihd,bmhjd->hbimj", query_blocks, key_slots, preferred_element_type=jnp.float32
    ) * HS ** (-0.5)
    valid_mask = my_valid[None, :, None, :, None]
    row_max = jnp.max(jnp.where(valid_mask, scores, -1e30), axis=(3, 4), keepdims=True)
    weights = jnp.where(valid_mask, jnp.exp(scores - row_max), 0.0)
    column_scale = jnp.ones(weights.shape[:2] + weights.shape[3:], jnp.float32)
    onehot = matches.astype(jnp.float32)
    for round_number in range(BALANCING_ROUNDS):
        row_scale = 1.0 / jnp.sum(weights * column_scale[:, :, None], axis=(3, 4))
        partial_cols = column_scale * jnp.sum(weights * row_scale[:, :, :, None, None], axis=2)
        column_complete = jnp.einsum(
            "bmt,hbmj->thj", onehot, partial_cols, precision=lax.Precision.HIGHEST
        ).reshape(seq_devices, local_blocks, heads_here, TILE)
        from_all = lax.all_to_all(
            column_complete, ("seq", "sub"), split_axis=0, concat_axis=0, tiled=True
        )
        owned_sums = jnp.sum(from_all, axis=0)
        spread = jnp.broadcast_to(owned_sums[None], (seq_devices,) + owned_sums.shape)
        totals = lax.all_to_all(
            spread, ("seq", "sub"), split_axis=0, concat_axis=0, tiled=True
        ).reshape(block_total, heads_here, TILE)
        per_slot = jnp.einsum("bmt,thj->hbmj", onehot, totals, precision=lax.Precision.HIGHEST)
        column_scale = column_scale / jnp.maximum(per_slot, COLUMN_FLOOR)
    probabilities = (
        weights * row_scale[:, :, :, None, None] * column_scale[:, :, None]
    ).astype(jnp.bfloat16)
    attended = jnp.einsum(
        "hbimj,bmhjd->bihd", probabilities, value_slots, preferred_element_type=jnp.float32
    )
    attended = attended.astype(jnp.bfloat16).reshape(row_count, heads_here * HS)
    head_count = lax.axis_size("head")
    if head_count != 2:
        partial_out = jnp.dot(attended, w_out, preferred_element_type=jnp.float32)
        return lax.psum_scatter(
            partial_out.astype(jnp.bfloat16), "head", scatter_dimension=1, tiled=True
        )
    head_index = lax.axis_index("head")
    width = w_out.shape[1] // 2
    other_cols = lax.dynamic_slice_in_dim(w_out, (1 - head_index) * width, width, 1)
    my_cols = lax.dynamic_slice_in_dim(w_out, head_index * width, width, 1)
    other_part = jnp.dot(attended, other_cols, preferred_element_type=jnp.float32)
    received = lax.ppermute(other_part.astype(jnp.bfloat16), "head", perm=[(0, 1), (1, 0)])
    my_part = jnp.dot(attended, my_cols, preferred_element_type=jnp.float32)
    return (my_part + received.astype(jnp.float32)).astype(jnp.bfloat16)


def solution(mesh):
    placed = (
        P(("groups", "seq", "sub"), None),
        P(None, "head"),
        P(None, "head"),
        P(None, "head"),
        P("head", None),
        P("groups", None),
        P("groups"),
    )
    return jax.shard_map(
        body,
        mesh=mesh,
        in_specs=placed,
        out_specs=P(("groups", "seq", "sub"), "head"),
        check_vma=False,
    )
```

```python
import jax
import jax.numpy as jnp
from jax import lax
from jax.sharding import PartitionSpec as P

HS = 128
TILE = 128
BALANCING_ROUNDS = 3


COLUMN_FLOOR = 0.1


def body(activations, w_query, w_key, w_value, w_out, tile_lists, query_block_counts):
    seq_devices = lax.axis_size(("seq", "sub"))
    device_index = lax.axis_index(("seq", "sub"))
    block_total = tile_lists.shape[0]
    maximum_tiles = tile_lists.shape[1]
    row_count = activations.shape[0]
    local_blocks = row_count // TILE
    heads_here = w_query.shape[1] // HS
    capacity = local_blocks * (maximum_tiles // 2) // seq_devices
    head_count = lax.axis_size("head")
    head_index = lax.axis_index("head")
    rows_part = TILE // head_count
    query_rows = jnp.dot(activations, w_query, preferred_element_type=jnp.float32).astype(
        jnp.bfloat16
    )
    act_tiles = activations.reshape(local_blocks, TILE, activations.shape[1])
    my_rows = lax.dynamic_slice_in_dim(act_tiles, head_index * rows_part, rows_part, 1)
    all_valid = jnp.arange(maximum_tiles, dtype=jnp.int32)[None, :] < query_block_counts[:, None]
    owned_ids = device_index * local_blocks + jnp.arange(local_blocks, dtype=jnp.int32)
    wanted = jnp.any(
        (tile_lists[:, :, None] == owned_ids[None, None, :]) & all_valid[:, :, None], axis=1
    )
    wanted = jnp.any(wanted.reshape(seq_devices, local_blocks, local_blocks), axis=1).astype(
        jnp.int32
    )
    slot_ranks = jnp.cumsum(wanted, axis=1) - wanted
    selector = (slot_ranks[:, None, :] == jnp.arange(capacity, dtype=jnp.int32)[None, :, None]) & (
        wanted[:, None, :] > 0
    )
    send_index = jnp.sum(
        selector.astype(jnp.int32) * jnp.arange(local_blocks, dtype=jnp.int32)[None, None, :], axis=2
    )
    my_lists = lax.dynamic_slice_in_dim(tile_lists, device_index * local_blocks, local_blocks, 0)
    my_valid = lax.dynamic_slice_in_dim(all_valid, device_index * local_blocks, local_blocks, 0)
    tile_ids = jnp.arange(block_total, dtype=jnp.int32)
    matches = (my_lists[:, :, None] == tile_ids[None, None, :]) & my_valid[:, :, None]
    requested = jnp.any(matches, axis=(0, 1)).astype(jnp.int32).reshape(seq_devices, local_blocks)
    own_ranks = jnp.cumsum(requested, axis=1) - requested
    sources = jnp.arange(seq_devices, dtype=jnp.int32)
    if seq_devices & (seq_devices - 1) == 0:
        source_steps = jnp.bitwise_xor(sources, device_index)
    else:
        source_steps = (device_index - sources) % seq_devices
    slot_table = (source_steps[:, None] * capacity + own_ranks).reshape(-1)
    slot_index = jnp.sum(jnp.where(matches, slot_table[None, None, :], 0), axis=2)
    key_weights = w_key.reshape(w_key.shape[0], heads_here, HS)
    value_weights = w_value.reshape(w_value.shape[0], heads_here, HS)
    power_of_two = seq_devices & (seq_devices - 1) == 0
    own_index = send_index[device_index]
    key_parts = {}
    value_parts = {}
    for step in sorted(range(seq_devices), key=lambda k: (k != 0, -k)):
        if step == 0:
            if head_count == 2:
                other_rows = lax.dynamic_slice_in_dim(
                    act_tiles, (1 - head_index) * rows_part, rows_part, 1
                )
                full = jnp.concatenate([my_rows, other_rows], axis=1)
            else:
                full = act_tiles
            full = jnp.take(full, own_index, axis=0, mode="clip")
        else:
            if power_of_two:
                target = jnp.bitwise_xor(device_index, step)
                pairs = [(i, i ^ step) for i in range(seq_devices)]
            else:
                target = (device_index + step) % seq_devices
                pairs = [(i, (i + step) % seq_devices) for i in range(seq_devices)]
            piece = jnp.take(my_rows, send_index[target], axis=0, mode="clip")
            got = lax.ppermute(piece, ("seq", "sub"), perm=pairs)
            if head_count == 2:
                partner = lax.ppermute(got, "head", perm=[(0, 1), (1, 0)])
                full = jnp.concatenate([got, partner], axis=1)
            else:
                full = lax.all_gather(got, "head", axis=1, tiled=True)
        key_parts[step] = jnp.einsum(
            "cjf,fhd->chjd", full, key_weights, preferred_element_type=jnp.float32
        ).astype(jnp.bfloat16)
        value_parts[step] = jnp.einsum(
            "cjf,fhd->chjd", full, value_weights, preferred_element_type=jnp.float32
        ).astype(jnp.bfloat16)
    key_all = jnp.concatenate([key_parts[k] for k in range(seq_devices)], axis=0)
    value_all = jnp.concatenate([value_parts[k] for k in range(seq_devices)], axis=0)
    flat_index = slot_index.reshape(-1)
    key_slots = jnp.take(key_all, flat_index, axis=0, mode="clip").reshape(
        local_blocks, maximum_tiles, heads_here, TILE, HS
    )
    value_slots = jnp.take(value_all, flat_index, axis=0, mode="clip").reshape(
        local_blocks, maximum_tiles, heads_here, TILE, HS
    )
    query_blocks = query_rows.reshape(local_blocks, TILE, heads_here, HS)
    scores = jnp.einsum(
        "bihd,bmhjd->hbimj", query_blocks, key_slots, preferred_element_type=jnp.float32
    ) * HS ** (-0.5)
    valid_mask = my_valid[None, :, None, :, None]
    row_max = jnp.max(jnp.where(valid_mask, scores, -1e30), axis=(3, 4), keepdims=True)
    weights = lax.optimization_barrier(jnp.where(valid_mask, jnp.exp(scores - row_max), 0.0))
    column_scale = jnp.ones(weights.shape[:2] + weights.shape[3:], jnp.float32)
    onehot = matches.astype(jnp.float32)
    for round_number in range(BALANCING_ROUNDS):
        row_scale = 1.0 / jnp.sum(weights * column_scale[:, :, None], axis=(3, 4))
        partial_cols = column_scale * jnp.sum(weights * row_scale[:, :, :, None, None], axis=2)
        column_complete = jnp.einsum(
            "bmt,hbmj->thj", onehot, partial_cols, precision=lax.Precision.HIGHEST
        ).reshape(seq_devices, local_blocks, heads_here, TILE)
        from_all = lax.all_to_all(
            column_complete, ("seq", "sub"), split_axis=0, concat_axis=0, tiled=True
        )
        owned_sums = jnp.sum(from_all, axis=0)
        spread = jnp.broadcast_to(owned_sums[None], (seq_devices,) + owned_sums.shape)
        totals = lax.all_to_all(
            spread, ("seq", "sub"), split_axis=0, concat_axis=0, tiled=True
        ).reshape(block_total, heads_here, TILE)
        per_slot = jnp.einsum("bmt,thj->hbmj", onehot, totals, precision=lax.Precision.HIGHEST)
        column_scale = column_scale / jnp.maximum(per_slot, COLUMN_FLOOR)
    probabilities = (
        weights * row_scale[:, :, :, None, None] * column_scale[:, :, None]
    ).astype(jnp.bfloat16)
    attended = jnp.einsum(
        "hbimj,bmhjd->bihd", probabilities, value_slots, preferred_element_type=jnp.float32
    )
    attended = attended.astype(jnp.bfloat16).reshape(row_count, heads_here * HS)
    head_count = lax.axis_size("head")
    if head_count != 2:
        partial_out = jnp.dot(attended, w_out, preferred_element_type=jnp.float32)
        return lax.psum_scatter(
            partial_out.astype(jnp.bfloat16), "head", scatter_dimension=1, tiled=True
        )
    head_index = lax.axis_index("head")
    width = w_out.shape[1] // 2
    other_cols = lax.dynamic_slice_in_dim(w_out, (1 - head_index) * width, width, 1)
    my_cols = lax.dynamic_slice_in_dim(w_out, head_index * width, width, 1)
    other_part = jnp.dot(attended, other_cols, preferred_element_type=jnp.float32)
    received = lax.ppermute(other_part.astype(jnp.bfloat16), "head", perm=[(0, 1), (1, 0)])
    my_part = jnp.dot(attended, my_cols, preferred_element_type=jnp.float32)
    return (my_part + received.astype(jnp.float32)).astype(jnp.bfloat16)


def solution(mesh):
    placed = (
        P(("groups", "seq", "sub"), None),
        P(None, "head"),
        P(None, "head"),
        P(None, "head"),
        P("head", None),
        P("groups", None),
        P("groups"),
    )
    return jax.shard_map(
        body,
        mesh=mesh,
        in_specs=placed,
        out_specs=P(("groups", "seq", "sub"), "head"),
        check_vma=False,
    )
```

```python
import jax
import jax.numpy as jnp
from jax import lax
from jax.experimental import pallas as pl
from jax.sharding import PartitionSpec as P

HS = 128
TILE = 128
BALANCING_ROUNDS = 3


COLUMN_FLOOR = 0.1


def round_kernel(score_ref, max_ref, valid_ref, column_ref, row_out, column_out):
    exps = jnp.where(valid_ref[0] > 0, jnp.exp(score_ref[0, 0] - max_ref[0, 0]), 0.0)
    column = column_ref[0, 0]
    row = 1.0 / jnp.sum(exps * column, axis=1, keepdims=True)
    row_out[0, 0] = row
    column_out[0, 0] = column * jnp.sum(exps * row, axis=0, keepdims=True)


def balance_round(scores, row_max, valid, column):
    heads, blocks, rows, width = scores.shape
    return pl.pallas_call(
        round_kernel,
        grid=(heads, blocks),
        in_specs=[
            pl.BlockSpec((1, 1, rows, width), lambda h, b: (h, b, 0, 0)),
            pl.BlockSpec((1, 1, rows, 1), lambda h, b: (h, b, 0, 0)),
            pl.BlockSpec((1, 1, width), lambda h, b: (b, 0, 0)),
            pl.BlockSpec((1, 1, 1, width), lambda h, b: (h, b, 0, 0)),
        ],
        out_specs=[
            pl.BlockSpec((1, 1, rows, 1), lambda h, b: (h, b, 0, 0)),
            pl.BlockSpec((1, 1, 1, width), lambda h, b: (h, b, 0, 0)),
        ],
        out_shape=[
            jax.ShapeDtypeStruct((heads, blocks, rows, 1), jnp.float32),
            jax.ShapeDtypeStruct((heads, blocks, 1, width), jnp.float32),
        ],
    )(scores, row_max, valid, column)


def body(activations, w_query, w_key, w_value, w_out, tile_lists, query_block_counts):
    seq_devices = lax.axis_size(("seq", "sub"))
    device_index = lax.axis_index(("seq", "sub"))
    block_total = tile_lists.shape[0]
    maximum_tiles = tile_lists.shape[1]
    row_count = activations.shape[0]
    local_blocks = row_count // TILE
    heads_here = w_query.shape[1] // HS
    capacity = local_blocks * (maximum_tiles // 2) // seq_devices
    head_count = lax.axis_size("head")
    head_index = lax.axis_index("head")
    rows_part = TILE // head_count
    query_rows = jnp.dot(activations, w_query, preferred_element_type=jnp.float32).astype(
        jnp.bfloat16
    )
    act_tiles = activations.reshape(local_blocks, TILE, activations.shape[1])
    my_rows = lax.dynamic_slice_in_dim(act_tiles, head_index * rows_part, rows_part, 1)
    all_valid = jnp.arange(maximum_tiles, dtype=jnp.int32)[None, :] < query_block_counts[:, None]
    owned_ids = device_index * local_blocks + jnp.arange(local_blocks, dtype=jnp.int32)
    wanted = jnp.any(
        (tile_lists[:, :, None] == owned_ids[None, None, :]) & all_valid[:, :, None], axis=1
    )
    wanted = jnp.any(wanted.reshape(seq_devices, local_blocks, local_blocks), axis=1).astype(
        jnp.int32
    )
    slot_ranks = jnp.cumsum(wanted, axis=1) - wanted
    selector = (slot_ranks[:, None, :] == jnp.arange(capacity, dtype=jnp.int32)[None, :, None]) & (
        wanted[:, None, :] > 0
    )
    send_index = jnp.sum(
        selector.astype(jnp.int32) * jnp.arange(local_blocks, dtype=jnp.int32)[None, None, :], axis=2
    )
    my_lists = lax.dynamic_slice_in_dim(tile_lists, device_index * local_blocks, local_blocks, 0)
    my_valid = lax.dynamic_slice_in_dim(all_valid, device_index * local_blocks, local_blocks, 0)
    tile_ids = jnp.arange(block_total, dtype=jnp.int32)
    matches = (my_lists[:, :, None] == tile_ids[None, None, :]) & my_valid[:, :, None]
    requested = jnp.any(matches, axis=(0, 1)).astype(jnp.int32).reshape(seq_devices, local_blocks)
    own_ranks = jnp.cumsum(requested, axis=1) - requested
    sources = jnp.arange(seq_devices, dtype=jnp.int32)
    if seq_devices & (seq_devices - 1) == 0:
        source_steps = jnp.bitwise_xor(sources, device_index)
    else:
        source_steps = (device_index - sources) % seq_devices
    slot_table = (source_steps[:, None] * capacity + own_ranks).reshape(-1)
    slot_index = jnp.sum(jnp.where(matches, slot_table[None, None, :], 0), axis=2)
    key_weights = w_key.reshape(w_key.shape[0], heads_here, HS)
    value_weights = w_value.reshape(w_value.shape[0], heads_here, HS)
    power_of_two = seq_devices & (seq_devices - 1) == 0
    own_index = send_index[device_index]
    key_parts = {}
    value_parts = {}
    for step in sorted(range(seq_devices), key=lambda k: (k != 0, -k)):
        if step == 0:
            if head_count == 2:
                other_rows = lax.dynamic_slice_in_dim(
                    act_tiles, (1 - head_index) * rows_part, rows_part, 1
                )
                full = jnp.concatenate([my_rows, other_rows], axis=1)
            else:
                full = act_tiles
            full = jnp.take(full, own_index, axis=0, mode="clip")
        else:
            if power_of_two:
                target = jnp.bitwise_xor(device_index, step)
                pairs = [(i, i ^ step) for i in range(seq_devices)]
            else:
                target = (device_index + step) % seq_devices
                pairs = [(i, (i + step) % seq_devices) for i in range(seq_devices)]
            piece = jnp.take(my_rows, send_index[target], axis=0, mode="clip")
            got = lax.ppermute(piece, ("seq", "sub"), perm=pairs)
            if head_count == 2:
                partner = lax.ppermute(got, "head", perm=[(0, 1), (1, 0)])
                full = jnp.concatenate([got, partner], axis=1)
            else:
                full = lax.all_gather(got, "head", axis=1, tiled=True)
        key_parts[step] = jnp.einsum(
            "cjf,fhd->chjd", full, key_weights, preferred_element_type=jnp.float32
        ).astype(jnp.bfloat16)
        value_parts[step] = jnp.einsum(
            "cjf,fhd->chjd", full, value_weights, preferred_element_type=jnp.float32
        ).astype(jnp.bfloat16)
    key_all = jnp.concatenate([key_parts[k] for k in range(seq_devices)], axis=0)
    value_all = jnp.concatenate([value_parts[k] for k in range(seq_devices)], axis=0)
    flat_index = slot_index.reshape(-1)
    key_slots = jnp.take(key_all, flat_index, axis=0, mode="clip").reshape(
        local_blocks, maximum_tiles, heads_here, TILE, HS
    )
    value_slots = jnp.take(value_all, flat_index, axis=0, mode="clip").reshape(
        local_blocks, maximum_tiles, heads_here, TILE, HS
    )
    query_blocks = query_rows.reshape(local_blocks, TILE, heads_here, HS)
    scores = jnp.einsum(
        "bihd,bmhjd->hbimj", query_blocks, key_slots, preferred_element_type=jnp.float32
    ) * HS ** (-0.5)
    valid_mask = my_valid[None, :, None, :, None]
    row_max = jnp.max(jnp.where(valid_mask, scores, -1e30), axis=(3, 4), keepdims=True)
    weights = jnp.where(valid_mask, jnp.exp(scores - row_max), 0.0)
    column_scale = jnp.ones(weights.shape[:2] + weights.shape[3:], jnp.float32)
    onehot = matches.astype(jnp.float32)
    slot_width = maximum_tiles * TILE
    flat_scores = scores.reshape(heads_here, local_blocks, TILE, slot_width)
    flat_max = row_max.reshape(heads_here, local_blocks, TILE, 1)
    flat_valid = jnp.repeat(my_valid.astype(jnp.float32), TILE, axis=1).reshape(
        local_blocks, 1, slot_width
    )
    for round_number in range(BALANCING_ROUNDS):
        row_out, column_out = balance_round(
            flat_scores,
            flat_max,
            flat_valid,
            column_scale.reshape(heads_here, local_blocks, 1, slot_width),
        )
        row_scale = row_out.reshape(heads_here, local_blocks, TILE)
        partial_cols = column_out.reshape(heads_here, local_blocks, maximum_tiles, TILE)
        column_complete = jnp.einsum(
            "bmt,hbmj->thj", onehot, partial_cols, precision=lax.Precision.HIGHEST
        ).reshape(seq_devices, local_blocks, heads_here, TILE)
        from_all = lax.all_to_all(
            column_complete, ("seq", "sub"), split_axis=0, concat_axis=0, tiled=True
        )
        owned_sums = jnp.sum(from_all, axis=0)
        spread = jnp.broadcast_to(owned_sums[None], (seq_devices,) + owned_sums.shape)
        totals = lax.all_to_all(
            spread, ("seq", "sub"), split_axis=0, concat_axis=0, tiled=True
        ).reshape(block_total, heads_here, TILE)
        per_slot = jnp.einsum("bmt,thj->hbmj", onehot, totals, precision=lax.Precision.HIGHEST)
        column_scale = column_scale / jnp.maximum(per_slot, COLUMN_FLOOR)
    probabilities = (
        weights * row_scale[:, :, :, None, None] * column_scale[:, :, None]
    ).astype(jnp.bfloat16)
    attended = jnp.einsum(
        "hbimj,bmhjd->bihd", probabilities, value_slots, preferred_element_type=jnp.float32
    )
    attended = attended.astype(jnp.bfloat16).reshape(row_count, heads_here * HS)
    head_count = lax.axis_size("head")
    if head_count != 2:
        partial_out = jnp.dot(attended, w_out, preferred_element_type=jnp.float32)
        return lax.psum_scatter(
            partial_out.astype(jnp.bfloat16), "head", scatter_dimension=1, tiled=True
        )
    head_index = lax.axis_index("head")
    width = w_out.shape[1] // 2
    other_cols = lax.dynamic_slice_in_dim(w_out, (1 - head_index) * width, width, 1)
    my_cols = lax.dynamic_slice_in_dim(w_out, head_index * width, width, 1)
    other_part = jnp.dot(attended, other_cols, preferred_element_type=jnp.float32)
    received = lax.ppermute(other_part.astype(jnp.bfloat16), "head", perm=[(0, 1), (1, 0)])
    my_part = jnp.dot(attended, my_cols, preferred_element_type=jnp.float32)
    return (my_part + received.astype(jnp.float32)).astype(jnp.bfloat16)


def solution(mesh):
    placed = (
        P(("groups", "seq", "sub"), None),
        P(None, "head"),
        P(None, "head"),
        P(None, "head"),
        P("head", None),
        P("groups", None),
        P("groups"),
    )
    return jax.shard_map(
        body,
        mesh=mesh,
        in_specs=placed,
        out_specs=P(("groups", "seq", "sub"), "head"),
        check_vma=False,
    )
```

```python
import jax
import jax.numpy as jnp
from jax import lax
from jax.sharding import PartitionSpec as P

HS = 128
TILE = 128
BALANCING_ROUNDS = 3


COLUMN_FLOOR = 0.1


def body(activations, w_query, w_key, w_value, w_out, tile_lists, query_block_counts):
    seq_devices = lax.axis_size(("seq", "sub"))
    device_index = lax.axis_index(("seq", "sub"))
    block_total = tile_lists.shape[0]
    maximum_tiles = tile_lists.shape[1]
    row_count = activations.shape[0]
    local_blocks = row_count // TILE
    heads_here = w_query.shape[1] // HS
    capacity = local_blocks * (maximum_tiles // 2) // seq_devices
    head_count = lax.axis_size("head")
    head_index = lax.axis_index("head")
    rows_part = TILE // head_count
    query_rows = jnp.dot(activations, w_query, preferred_element_type=jnp.float32).astype(
        jnp.bfloat16
    )
    act_tiles = activations.reshape(local_blocks, TILE, activations.shape[1])
    my_rows = lax.dynamic_slice_in_dim(act_tiles, head_index * rows_part, rows_part, 1)
    all_valid = jnp.arange(maximum_tiles, dtype=jnp.int32)[None, :] < query_block_counts[:, None]
    owned_ids = device_index * local_blocks + jnp.arange(local_blocks, dtype=jnp.int32)
    wanted = jnp.any(
        (tile_lists[:, :, None] == owned_ids[None, None, :]) & all_valid[:, :, None], axis=1
    )
    wanted = jnp.any(wanted.reshape(seq_devices, local_blocks, local_blocks), axis=1).astype(
        jnp.int32
    )
    slot_ranks = jnp.cumsum(wanted, axis=1) - wanted
    selector = (slot_ranks[:, None, :] == jnp.arange(capacity, dtype=jnp.int32)[None, :, None]) & (
        wanted[:, None, :] > 0
    )
    send_index = jnp.sum(
        selector.astype(jnp.int32) * jnp.arange(local_blocks, dtype=jnp.int32)[None, None, :], axis=2
    )
    my_lists = lax.dynamic_slice_in_dim(tile_lists, device_index * local_blocks, local_blocks, 0)
    my_valid = lax.dynamic_slice_in_dim(all_valid, device_index * local_blocks, local_blocks, 0)
    tile_ids = jnp.arange(block_total, dtype=jnp.int32)
    matches = (my_lists[:, :, None] == tile_ids[None, None, :]) & my_valid[:, :, None]
    requested = jnp.any(matches, axis=(0, 1)).astype(jnp.int32).reshape(seq_devices, local_blocks)
    own_ranks = jnp.cumsum(requested, axis=1) - requested
    sources = jnp.arange(seq_devices, dtype=jnp.int32)
    if seq_devices & (seq_devices - 1) == 0:
        source_steps = jnp.bitwise_xor(sources, device_index)
    else:
        source_steps = (device_index - sources) % seq_devices
    slot_table = (source_steps[:, None] * capacity + own_ranks).reshape(-1)
    slot_index = jnp.sum(jnp.where(matches, slot_table[None, None, :], 0), axis=2)
    key_weights = w_key.reshape(w_key.shape[0], heads_here, HS)
    value_weights = w_value.reshape(w_value.shape[0], heads_here, HS)
    power_of_two = seq_devices & (seq_devices - 1) == 0
    own_index = send_index[device_index]
    later_steps = jnp.arange(1, seq_devices, dtype=jnp.int32)
    if power_of_two:
        step_targets = jnp.bitwise_xor(device_index, later_steps)
    else:
        step_targets = (device_index + later_steps) % seq_devices
    step_pieces = jnp.take(
        my_rows, jnp.take(send_index, step_targets, axis=0).reshape(-1), axis=0, mode="clip"
    ).reshape(seq_devices - 1, capacity, rows_part, my_rows.shape[2])
    key_parts = {}
    value_parts = {}
    for step in sorted(range(seq_devices), key=lambda k: (k != 0, -k)):
        if step == 0:
            if head_count == 2:
                other_rows = lax.dynamic_slice_in_dim(
                    act_tiles, (1 - head_index) * rows_part, rows_part, 1
                )
                full = jnp.concatenate([my_rows, other_rows], axis=1)
            else:
                full = act_tiles
            full = jnp.take(full, own_index, axis=0, mode="clip")
        else:
            if power_of_two:
                target = jnp.bitwise_xor(device_index, step)
                pairs = [(i, i ^ step) for i in range(seq_devices)]
            else:
                target = (device_index + step) % seq_devices
                pairs = [(i, (i + step) % seq_devices) for i in range(seq_devices)]
            piece = step_pieces[step - 1]
            got = lax.ppermute(piece, ("seq", "sub"), perm=pairs)
            if head_count == 2:
                partner = lax.ppermute(got, "head", perm=[(0, 1), (1, 0)])
                full = jnp.concatenate([got, partner], axis=1)
            else:
                full = lax.all_gather(got, "head", axis=1, tiled=True)
        key_parts[step] = jnp.einsum(
            "cjf,fhd->chjd", full, key_weights, preferred_element_type=jnp.float32
        ).astype(jnp.bfloat16)
        value_parts[step] = jnp.einsum(
            "cjf,fhd->chjd", full, value_weights, preferred_element_type=jnp.float32
        ).astype(jnp.bfloat16)
    key_all = jnp.concatenate([key_parts[k] for k in range(seq_devices)], axis=0)
    value_all = jnp.concatenate([value_parts[k] for k in range(seq_devices)], axis=0)
    flat_index = slot_index.reshape(-1)
    key_slots = jnp.take(key_all, flat_index, axis=0, mode="clip").reshape(
        local_blocks, maximum_tiles, heads_here, TILE, HS
    )
    value_slots = jnp.take(value_all, flat_index, axis=0, mode="clip").reshape(
        local_blocks, maximum_tiles, heads_here, TILE, HS
    )
    query_blocks = query_rows.reshape(local_blocks, TILE, heads_here, HS)
    scores = jnp.einsum(
        "bihd,bmhjd->hbimj", query_blocks, key_slots, preferred_element_type=jnp.float32
    ) * HS ** (-0.5)
    valid_mask = my_valid[None, :, None, :, None]
    row_max = jnp.max(jnp.where(valid_mask, scores, -1e30), axis=(3, 4), keepdims=True)
    weights = jnp.where(valid_mask, jnp.exp(scores - row_max), 0.0)
    column_scale = jnp.ones(weights.shape[:2] + weights.shape[3:], jnp.float32)
    onehot = matches.astype(jnp.float32)
    for round_number in range(BALANCING_ROUNDS):
        row_scale = 1.0 / jnp.sum(weights * column_scale[:, :, None], axis=(3, 4))
        partial_cols = column_scale * jnp.sum(weights * row_scale[:, :, :, None, None], axis=2)
        column_complete = jnp.einsum(
            "bmt,hbmj->thj", onehot, partial_cols, precision=lax.Precision.HIGHEST
        ).reshape(seq_devices, local_blocks, heads_here, TILE)
        from_all = lax.all_to_all(
            column_complete, ("seq", "sub"), split_axis=0, concat_axis=0, tiled=True
        )
        owned_sums = jnp.sum(from_all, axis=0)
        spread = jnp.broadcast_to(owned_sums[None], (seq_devices,) + owned_sums.shape)
        totals = lax.all_to_all(
            spread, ("seq", "sub"), split_axis=0, concat_axis=0, tiled=True
        ).reshape(block_total, heads_here, TILE)
        per_slot = jnp.einsum("bmt,thj->hbmj", onehot, totals, precision=lax.Precision.HIGHEST)
        column_scale = column_scale / jnp.maximum(per_slot, COLUMN_FLOOR)
    probabilities = (
        weights * row_scale[:, :, :, None, None] * column_scale[:, :, None]
    ).astype(jnp.bfloat16)
    attended = jnp.einsum(
        "hbimj,bmhjd->bihd", probabilities, value_slots, preferred_element_type=jnp.float32
    )
    attended = attended.astype(jnp.bfloat16).reshape(row_count, heads_here * HS)
    head_count = lax.axis_size("head")
    if head_count != 2:
        partial_out = jnp.dot(attended, w_out, preferred_element_type=jnp.float32)
        return lax.psum_scatter(
            partial_out.astype(jnp.bfloat16), "head", scatter_dimension=1, tiled=True
        )
    head_index = lax.axis_index("head")
    width = w_out.shape[1] // 2
    other_cols = lax.dynamic_slice_in_dim(w_out, (1 - head_index) * width, width, 1)
    my_cols = lax.dynamic_slice_in_dim(w_out, head_index * width, width, 1)
    other_part = jnp.dot(attended, other_cols, preferred_element_type=jnp.float32)
    received = lax.ppermute(other_part.astype(jnp.bfloat16), "head", perm=[(0, 1), (1, 0)])
    my_part = jnp.dot(attended, my_cols, preferred_element_type=jnp.float32)
    return (my_part + received.astype(jnp.float32)).astype(jnp.bfloat16)


def solution(mesh):
    placed = (
        P(("groups", "seq", "sub"), None),
        P(None, "head"),
        P(None, "head"),
        P(None, "head"),
        P("head", None),
        P("groups", None),
        P("groups"),
    )
    return jax.shard_map(
        body,
        mesh=mesh,
        in_specs=placed,
        out_specs=P(("groups", "seq", "sub"), "head"),
        check_vma=False,
    )
```

```python
import jax
import jax.numpy as jnp
from jax import lax
from jax.sharding import PartitionSpec as P

HS = 128
TILE = 128
BALANCING_ROUNDS = 3


COLUMN_FLOOR = 0.1


def body(activations, w_query, w_key, w_value, w_out, tile_lists, query_block_counts):
    seq_devices = lax.axis_size(("seq", "sub"))
    device_index = lax.axis_index(("seq", "sub"))
    block_total = tile_lists.shape[0]
    maximum_tiles = tile_lists.shape[1]
    row_count = activations.shape[0]
    local_blocks = row_count // TILE
    heads_here = w_query.shape[1] // HS
    capacity = local_blocks * (maximum_tiles // 2) // seq_devices
    head_count = lax.axis_size("head")
    head_index = lax.axis_index("head")
    rows_part = TILE // head_count
    query_rows = jnp.dot(activations, w_query, preferred_element_type=jnp.float32).astype(
        jnp.bfloat16
    )
    act_tiles = activations.reshape(local_blocks, TILE, activations.shape[1])
    my_rows = lax.dynamic_slice_in_dim(act_tiles, head_index * rows_part, rows_part, 1)
    all_valid = jnp.arange(maximum_tiles, dtype=jnp.int32)[None, :] < query_block_counts[:, None]
    owned_ids = device_index * local_blocks + jnp.arange(local_blocks, dtype=jnp.int32)
    wanted = jnp.any(
        (tile_lists[:, :, None] == owned_ids[None, None, :]) & all_valid[:, :, None], axis=1
    )
    wanted = jnp.any(wanted.reshape(seq_devices, local_blocks, local_blocks), axis=1).astype(
        jnp.int32
    )
    slot_ranks = jnp.cumsum(wanted, axis=1) - wanted
    selector = (slot_ranks[:, None, :] == jnp.arange(capacity, dtype=jnp.int32)[None, :, None]) & (
        wanted[:, None, :] > 0
    )
    send_index = jnp.sum(
        selector.astype(jnp.int32) * jnp.arange(local_blocks, dtype=jnp.int32)[None, None, :], axis=2
    )
    my_lists = lax.dynamic_slice_in_dim(tile_lists, device_index * local_blocks, local_blocks, 0)
    my_valid = lax.dynamic_slice_in_dim(all_valid, device_index * local_blocks, local_blocks, 0)
    tile_ids = jnp.arange(block_total, dtype=jnp.int32)
    matches = (my_lists[:, :, None] == tile_ids[None, None, :]) & my_valid[:, :, None]
    requested = jnp.any(matches, axis=(0, 1)).astype(jnp.int32).reshape(seq_devices, local_blocks)
    own_ranks = jnp.cumsum(requested, axis=1) - requested
    sources = jnp.arange(seq_devices, dtype=jnp.int32)
    if seq_devices & (seq_devices - 1) == 0:
        source_steps = jnp.bitwise_xor(sources, device_index)
    else:
        source_steps = (device_index - sources) % seq_devices
    slot_table = (source_steps[:, None] * capacity + own_ranks).reshape(-1)
    slot_index = jnp.sum(jnp.where(matches, slot_table[None, None, :], 0), axis=2)
    key_weights = w_key.reshape(w_key.shape[0], heads_here, HS)
    value_weights = w_value.reshape(w_value.shape[0], heads_here, HS)
    power_of_two = seq_devices & (seq_devices - 1) == 0
    own_index = send_index[device_index]
    direct_steps = 2 if seq_devices > 2 else 1
    later_steps = jnp.arange(direct_steps, seq_devices, dtype=jnp.int32)
    if power_of_two:
        step_targets = jnp.bitwise_xor(device_index, later_steps)
    else:
        step_targets = (device_index + later_steps) % seq_devices
    step_pieces = jnp.take(
        my_rows, jnp.take(send_index, step_targets, axis=0).reshape(-1), axis=0, mode="clip"
    ).reshape(seq_devices - direct_steps, capacity, rows_part, my_rows.shape[2])
    if head_count == 2:
        other_rows = lax.dynamic_slice_in_dim(act_tiles, (1 - head_index) * rows_part, rows_part, 1)
        own_full = jnp.concatenate([my_rows, other_rows], axis=1)
    else:
        own_full = act_tiles
    key_parts = {}
    value_parts = {}
    for step in sorted(range(seq_devices), key=lambda k: (k != 0, -k)):
        if power_of_two:
            target = jnp.bitwise_xor(device_index, step)
            pairs = [(i, i ^ step) for i in range(seq_devices)]
        else:
            target = (device_index + step) % seq_devices
            pairs = [(i, (i + step) % seq_devices) for i in range(seq_devices)]
        if step == 0:
            full = jnp.take(own_full, own_index, axis=0, mode="clip")
        elif step < direct_steps:
            sent = jnp.take(own_full, send_index[target], axis=0, mode="clip")
            sent_keys = jnp.einsum(
                "cjf,fhd->chjd", sent, key_weights, preferred_element_type=jnp.float32
            ).astype(jnp.bfloat16)
            sent_values = jnp.einsum(
                "cjf,fhd->chjd", sent, value_weights, preferred_element_type=jnp.float32
            ).astype(jnp.bfloat16)
            both = lax.ppermute(
                jnp.stack([sent_keys, sent_values]), ("seq", "sub"), perm=pairs
            )
            key_parts[step] = both[0]
            value_parts[step] = both[1]
            continue
        else:
            piece = step_pieces[step - direct_steps]
            got = lax.ppermute(piece, ("seq", "sub"), perm=pairs)
            if head_count == 2:
                partner = lax.ppermute(got, "head", perm=[(0, 1), (1, 0)])
                full = jnp.concatenate([got, partner], axis=1)
            else:
                full = lax.all_gather(got, "head", axis=1, tiled=True)
        key_parts[step] = jnp.einsum(
            "cjf,fhd->chjd", full, key_weights, preferred_element_type=jnp.float32
        ).astype(jnp.bfloat16)
        value_parts[step] = jnp.einsum(
            "cjf,fhd->chjd", full, value_weights, preferred_element_type=jnp.float32
        ).astype(jnp.bfloat16)
    key_all = jnp.concatenate([key_parts[k] for k in range(seq_devices)], axis=0)
    value_all = jnp.concatenate([value_parts[k] for k in range(seq_devices)], axis=0)
    flat_index = slot_index.reshape(-1)
    key_slots = jnp.take(key_all, flat_index, axis=0, mode="clip").reshape(
        local_blocks, maximum_tiles, heads_here, TILE, HS
    )
    value_slots = jnp.take(value_all, flat_index, axis=0, mode="clip").reshape(
        local_blocks, maximum_tiles, heads_here, TILE, HS
    )
    query_blocks = query_rows.reshape(local_blocks, TILE, heads_here, HS)
    scores = jnp.einsum(
        "bihd,bmhjd->hbimj", query_blocks, key_slots, preferred_element_type=jnp.float32
    ) * HS ** (-0.5)
    valid_mask = my_valid[None, :, None, :, None]
    row_max = jnp.max(jnp.where(valid_mask, scores, -1e30), axis=(3, 4), keepdims=True)
    weights = jnp.where(valid_mask, jnp.exp(scores - row_max), 0.0)
    column_scale = jnp.ones(weights.shape[:2] + weights.shape[3:], jnp.float32)
    onehot = matches.astype(jnp.float32)
    for round_number in range(BALANCING_ROUNDS):
        row_scale = 1.0 / jnp.sum(weights * column_scale[:, :, None], axis=(3, 4))
        partial_cols = column_scale * jnp.sum(weights * row_scale[:, :, :, None, None], axis=2)
        column_complete = jnp.einsum(
            "bmt,hbmj->thj", onehot, partial_cols, precision=lax.Precision.HIGHEST
        ).reshape(seq_devices, local_blocks, heads_here, TILE)
        from_all = lax.all_to_all(
            column_complete, ("seq", "sub"), split_axis=0, concat_axis=0, tiled=True
        )
        owned_sums = jnp.sum(from_all, axis=0)
        spread = jnp.broadcast_to(owned_sums[None], (seq_devices,) + owned_sums.shape)
        totals = lax.all_to_all(
            spread, ("seq", "sub"), split_axis=0, concat_axis=0, tiled=True
        ).reshape(block_total, heads_here, TILE)
        per_slot = jnp.einsum("bmt,thj->hbmj", onehot, totals, precision=lax.Precision.HIGHEST)
        column_scale = column_scale / jnp.maximum(per_slot, COLUMN_FLOOR)
    probabilities = (
        weights * row_scale[:, :, :, None, None] * column_scale[:, :, None]
    ).astype(jnp.bfloat16)
    attended = jnp.einsum(
        "hbimj,bmhjd->bihd", probabilities, value_slots, preferred_element_type=jnp.float32
    )
    attended = attended.astype(jnp.bfloat16).reshape(row_count, heads_here * HS)
    head_count = lax.axis_size("head")
    if head_count != 2:
        partial_out = jnp.dot(attended, w_out, preferred_element_type=jnp.float32)
        return lax.psum_scatter(
            partial_out.astype(jnp.bfloat16), "head", scatter_dimension=1, tiled=True
        )
    head_index = lax.axis_index("head")
    width = w_out.shape[1] // 2
    other_cols = lax.dynamic_slice_in_dim(w_out, (1 - head_index) * width, width, 1)
    my_cols = lax.dynamic_slice_in_dim(w_out, head_index * width, width, 1)
    other_part = jnp.dot(attended, other_cols, preferred_element_type=jnp.float32)
    received = lax.ppermute(other_part.astype(jnp.bfloat16), "head", perm=[(0, 1), (1, 0)])
    my_part = jnp.dot(attended, my_cols, preferred_element_type=jnp.float32)
    return (my_part + received.astype(jnp.float32)).astype(jnp.bfloat16)


def solution(mesh):
    placed = (
        P(("groups", "seq", "sub"), None),
        P(None, "head"),
        P(None, "head"),
        P(None, "head"),
        P("head", None),
        P("groups", None),
        P("groups"),
    )
    return jax.shard_map(
        body,
        mesh=mesh,
        in_specs=placed,
        out_specs=P(("groups", "seq", "sub"), "head"),
        check_vma=False,
    )
```

```python
import jax
import jax.numpy as jnp
from jax import lax
from jax.sharding import PartitionSpec as P

HS = 128
TILE = 128
BALANCING_ROUNDS = 3


COLUMN_FLOOR = 0.1


def body(activations, w_query, w_key, w_value, w_out, tile_lists, query_block_counts):
    seq_devices = lax.axis_size(("seq", "sub"))
    device_index = lax.axis_index(("seq", "sub"))
    block_total = tile_lists.shape[0]
    maximum_tiles = tile_lists.shape[1]
    row_count = activations.shape[0]
    local_blocks = row_count // TILE
    heads_here = w_query.shape[1] // HS
    capacity = local_blocks * (maximum_tiles // 2) // seq_devices
    head_count = lax.axis_size("head")
    head_index = lax.axis_index("head")
    rows_part = TILE // head_count
    query_rows = jnp.dot(activations, w_query, preferred_element_type=jnp.float32).astype(
        jnp.bfloat16
    )
    act_tiles = activations.reshape(local_blocks, TILE, activations.shape[1])
    my_rows = lax.dynamic_slice_in_dim(act_tiles, head_index * rows_part, rows_part, 1)
    all_valid = jnp.arange(maximum_tiles, dtype=jnp.int32)[None, :] < query_block_counts[:, None]
    owned_ids = device_index * local_blocks + jnp.arange(local_blocks, dtype=jnp.int32)
    wanted = jnp.any(
        (tile_lists[:, :, None] == owned_ids[None, None, :]) & all_valid[:, :, None], axis=1
    )
    wanted = jnp.any(wanted.reshape(seq_devices, local_blocks, local_blocks), axis=1).astype(
        jnp.int32
    )
    slot_ranks = jnp.cumsum(wanted, axis=1) - wanted
    selector = (slot_ranks[:, None, :] == jnp.arange(capacity, dtype=jnp.int32)[None, :, None]) & (
        wanted[:, None, :] > 0
    )
    send_index = jnp.sum(
        selector.astype(jnp.int32) * jnp.arange(local_blocks, dtype=jnp.int32)[None, None, :], axis=2
    )
    my_lists = lax.dynamic_slice_in_dim(tile_lists, device_index * local_blocks, local_blocks, 0)
    my_valid = lax.dynamic_slice_in_dim(all_valid, device_index * local_blocks, local_blocks, 0)
    tile_ids = jnp.arange(block_total, dtype=jnp.int32)
    matches = (my_lists[:, :, None] == tile_ids[None, None, :]) & my_valid[:, :, None]
    requested = jnp.any(matches, axis=(0, 1)).astype(jnp.int32).reshape(seq_devices, local_blocks)
    own_ranks = jnp.cumsum(requested, axis=1) - requested
    sources = jnp.arange(seq_devices, dtype=jnp.int32)
    if seq_devices & (seq_devices - 1) == 0:
        source_steps = jnp.bitwise_xor(sources, device_index)
    else:
        source_steps = (device_index - sources) % seq_devices
    slot_table = (source_steps[:, None] * capacity + own_ranks).reshape(-1)
    slot_index = jnp.sum(jnp.where(matches, slot_table[None, None, :], 0), axis=2)
    key_weights = w_key.reshape(w_key.shape[0], heads_here, HS)
    value_weights = w_value.reshape(w_value.shape[0], heads_here, HS)
    power_of_two = seq_devices & (seq_devices - 1) == 0
    own_index = send_index[device_index]
    later_steps = jnp.arange(1, seq_devices, dtype=jnp.int32)
    if power_of_two:
        step_targets = jnp.bitwise_xor(device_index, later_steps)
    else:
        step_targets = (device_index + later_steps) % seq_devices
    step_pieces = jnp.take(
        my_rows, jnp.take(send_index, step_targets, axis=0).reshape(-1), axis=0, mode="clip"
    ).reshape(seq_devices - 1, capacity, rows_part, my_rows.shape[2])
    key_parts = {}
    value_parts = {}
    for step in sorted(range(seq_devices), key=lambda k: (k != 0, -k)):
        if step == 0:
            if head_count == 2:
                other_rows = lax.dynamic_slice_in_dim(
                    act_tiles, (1 - head_index) * rows_part, rows_part, 1
                )
                full = jnp.concatenate([my_rows, other_rows], axis=1)
            else:
                full = act_tiles
            full = jnp.take(full, own_index, axis=0, mode="clip")
        else:
            if power_of_two:
                target = jnp.bitwise_xor(device_index, step)
                pairs = [(i, i ^ step) for i in range(seq_devices)]
            else:
                target = (device_index + step) % seq_devices
                pairs = [(i, (i + step) % seq_devices) for i in range(seq_devices)]
            piece = step_pieces[step - 1]
            got = lax.ppermute(piece, ("seq", "sub"), perm=pairs)
            if head_count == 2:
                partner = lax.ppermute(got, "head", perm=[(0, 1), (1, 0)])
                full = jnp.concatenate([got, partner], axis=1)
            else:
                full = lax.all_gather(got, "head", axis=1, tiled=True)
        key_parts[step] = jnp.einsum(
            "cjf,fhd->chjd", full, key_weights, preferred_element_type=jnp.float32
        ).astype(jnp.bfloat16)
        value_parts[step] = jnp.einsum(
            "cjf,fhd->chjd", full, value_weights, preferred_element_type=jnp.float32
        ).astype(jnp.bfloat16)
    key_all = jnp.concatenate([key_parts[k] for k in range(seq_devices)], axis=0)
    value_all = jnp.concatenate([value_parts[k] for k in range(seq_devices)], axis=0)
    flat_index = slot_index.reshape(-1)
    key_slots = jnp.take(key_all, flat_index, axis=0, mode="clip").reshape(
        local_blocks, maximum_tiles, heads_here, TILE, HS
    )
    value_slots = jnp.take(value_all, flat_index, axis=0, mode="clip").reshape(
        local_blocks, maximum_tiles, heads_here, TILE, HS
    )
    query_blocks = query_rows.reshape(local_blocks, TILE, heads_here, HS)
    scores = jnp.einsum(
        "bihd,bmhjd->hbimj", query_blocks, key_slots, preferred_element_type=jnp.float32
    ) * HS ** (-0.5)
    valid_mask = my_valid[None, :, None, :, None]
    row_max = jnp.max(jnp.where(valid_mask, scores, -1e30), axis=(3, 4), keepdims=True)
    weights = jnp.where(valid_mask, jnp.exp(scores - row_max), 0.0)
    column_scale = jnp.ones(weights.shape[:2] + weights.shape[3:], jnp.float32)
    onehot = matches.astype(jnp.float32)
    for round_number in range(BALANCING_ROUNDS):
        row_scale = 1.0 / jnp.sum(weights * column_scale[:, :, None], axis=(3, 4))
        partial_cols = column_scale * jnp.sum(weights * row_scale[:, :, :, None, None], axis=2)
        column_complete = jnp.einsum(
            "bmt,hbmj->thj", onehot, partial_cols, precision=lax.Precision.HIGHEST
        ).reshape(seq_devices, local_blocks, heads_here, TILE)
        from_all = lax.all_to_all(
            column_complete, ("seq", "sub"), split_axis=0, concat_axis=0, tiled=True
        )
        owned_sums = jnp.sum(from_all, axis=0)
        spread = jnp.broadcast_to(owned_sums[None], (seq_devices,) + owned_sums.shape)
        totals = lax.all_to_all(
            spread, ("seq", "sub"), split_axis=0, concat_axis=0, tiled=True
        ).reshape(block_total, heads_here, TILE)
        per_slot = jnp.einsum("bmt,thj->hbmj", onehot, totals, precision=lax.Precision.HIGHEST)
        column_scale = column_scale / jnp.maximum(per_slot, COLUMN_FLOOR)
    head_count = lax.axis_size("head")

    def attend(first, last):
        probabilities = (
            jnp.where(
                valid_mask[:, first:last],
                jnp.exp(scores[:, first:last] - row_max[:, first:last]),
                0.0,
            )
            * row_scale[:, first:last, :, None, None]
            * column_scale[:, first:last, None]
        ).astype(jnp.bfloat16)
        attended = jnp.einsum(
            "hbimj,bmhjd->bihd",
            probabilities,
            value_slots[first:last],
            preferred_element_type=jnp.float32,
        )
        return attended.astype(jnp.bfloat16).reshape((last - first) * TILE, heads_here * HS)

    if head_count != 2:
        partial_out = jnp.dot(attend(0, local_blocks), w_out, preferred_element_type=jnp.float32)
        return lax.psum_scatter(
            partial_out.astype(jnp.bfloat16), "head", scatter_dimension=1, tiled=True
        )
    head_index = lax.axis_index("head")
    width = w_out.shape[1] // 2
    other_cols = lax.dynamic_slice_in_dim(w_out, (1 - head_index) * width, width, 1)
    my_cols = lax.dynamic_slice_in_dim(w_out, head_index * width, width, 1)
    pieces = 2 if local_blocks % 2 == 0 else 1
    piece_blocks = local_blocks // pieces
    outputs = []
    for piece_number in range(pieces):
        attended = attend(piece_number * piece_blocks, (piece_number + 1) * piece_blocks)
        other_part = jnp.dot(attended, other_cols, preferred_element_type=jnp.float32)
        received = lax.ppermute(other_part.astype(jnp.bfloat16), "head", perm=[(0, 1), (1, 0)])
        my_part = jnp.dot(attended, my_cols, preferred_element_type=jnp.float32)
        outputs.append((my_part + received.astype(jnp.float32)).astype(jnp.bfloat16))
    return jnp.concatenate(outputs, axis=0)


def solution(mesh):
    placed = (
        P(("groups", "seq", "sub"), None),
        P(None, "head"),
        P(None, "head"),
        P(None, "head"),
        P("head", None),
        P("groups", None),
        P("groups"),
    )
    return jax.shard_map(
        body,
        mesh=mesh,
        in_specs=placed,
        out_specs=P(("groups", "seq", "sub"), "head"),
        check_vma=False,
    )
```

```python
import jax
import jax.numpy as jnp
from jax import lax
from jax.sharding import PartitionSpec as P

HS = 128
TILE = 128
BALANCING_ROUNDS = 3


COLUMN_FLOOR = 0.1


def body(activations, w_query, w_key, w_value, w_out, tile_lists, query_block_counts):
    seq_devices = lax.axis_size(("seq", "sub"))
    device_index = lax.axis_index(("seq", "sub"))
    block_total = tile_lists.shape[0]
    maximum_tiles = tile_lists.shape[1]
    row_count = activations.shape[0]
    local_blocks = row_count // TILE
    heads_here = w_query.shape[1] // HS
    capacity = local_blocks * (maximum_tiles // 2) // seq_devices
    head_count = lax.axis_size("head")
    head_index = lax.axis_index("head")
    rows_part = TILE // head_count
    query_rows = jnp.dot(activations, w_query, preferred_element_type=jnp.float32).astype(
        jnp.bfloat16
    )
    act_tiles = activations.reshape(local_blocks, TILE, activations.shape[1])
    my_rows = lax.dynamic_slice_in_dim(act_tiles, head_index * rows_part, rows_part, 1)
    all_valid = jnp.arange(maximum_tiles, dtype=jnp.int32)[None, :] < query_block_counts[:, None]
    owned_ids = device_index * local_blocks + jnp.arange(local_blocks, dtype=jnp.int32)
    wanted = jnp.any(
        (tile_lists[:, :, None] == owned_ids[None, None, :]) & all_valid[:, :, None], axis=1
    )
    wanted = jnp.any(wanted.reshape(seq_devices, local_blocks, local_blocks), axis=1).astype(
        jnp.int32
    )
    slot_ranks = jnp.cumsum(wanted, axis=1) - wanted
    selector = (slot_ranks[:, None, :] == jnp.arange(capacity, dtype=jnp.int32)[None, :, None]) & (
        wanted[:, None, :] > 0
    )
    send_index = jnp.sum(
        selector.astype(jnp.int32) * jnp.arange(local_blocks, dtype=jnp.int32)[None, None, :], axis=2
    )
    my_lists = lax.dynamic_slice_in_dim(tile_lists, device_index * local_blocks, local_blocks, 0)
    my_valid = lax.dynamic_slice_in_dim(all_valid, device_index * local_blocks, local_blocks, 0)
    tile_ids = jnp.arange(block_total, dtype=jnp.int32)
    matches = (my_lists[:, :, None] == tile_ids[None, None, :]) & my_valid[:, :, None]
    requested = jnp.any(matches, axis=(0, 1)).astype(jnp.int32).reshape(seq_devices, local_blocks)
    own_ranks = jnp.cumsum(requested, axis=1) - requested
    sources = jnp.arange(seq_devices, dtype=jnp.int32)
    if seq_devices & (seq_devices - 1) == 0:
        source_steps = jnp.bitwise_xor(sources, device_index)
    else:
        source_steps = (device_index - sources) % seq_devices
    slot_table = (source_steps[:, None] * capacity + own_ranks).reshape(-1)
    slot_index = jnp.sum(jnp.where(matches, slot_table[None, None, :], 0), axis=2)
    key_weights = w_key.reshape(w_key.shape[0], heads_here, HS)
    value_weights = w_value.reshape(w_value.shape[0], heads_here, HS)
    power_of_two = seq_devices & (seq_devices - 1) == 0
    own_index = send_index[device_index]
    later_steps = jnp.arange(1, seq_devices, dtype=jnp.int32)
    if power_of_two:
        step_targets = jnp.bitwise_xor(device_index, later_steps)
    else:
        step_targets = (device_index + later_steps) % seq_devices
    step_indices = jnp.take(send_index, step_targets, axis=0)
    key_parts = {}
    value_parts = {}
    for step in sorted(range(seq_devices), key=lambda k: (k != 0, -k)):
        if step == 0:
            if head_count == 2:
                other_rows = lax.dynamic_slice_in_dim(
                    act_tiles, (1 - head_index) * rows_part, rows_part, 1
                )
                full = jnp.concatenate([my_rows, other_rows], axis=1)
            else:
                full = act_tiles
            full = jnp.take(full, own_index, axis=0, mode="clip")
        else:
            if power_of_two:
                target = jnp.bitwise_xor(device_index, step)
                pairs = [(i, i ^ step) for i in range(seq_devices)]
            else:
                target = (device_index + step) % seq_devices
                pairs = [(i, (i + step) % seq_devices) for i in range(seq_devices)]
            piece = jnp.stack(
                [
                    lax.dynamic_index_in_dim(
                        my_rows, step_indices[step - 1, slot], axis=0, keepdims=False
                    )
                    for slot in range(capacity)
                ]
            )
            got = lax.ppermute(piece, ("seq", "sub"), perm=pairs)
            if head_count == 2:
                partner = lax.ppermute(got, "head", perm=[(0, 1), (1, 0)])
                full = jnp.concatenate([got, partner], axis=1)
            else:
                full = lax.all_gather(got, "head", axis=1, tiled=True)
        key_parts[step] = jnp.einsum(
            "cjf,fhd->chjd", full, key_weights, preferred_element_type=jnp.float32
        ).astype(jnp.bfloat16)
        value_parts[step] = jnp.einsum(
            "cjf,fhd->chjd", full, value_weights, preferred_element_type=jnp.float32
        ).astype(jnp.bfloat16)
    key_all = jnp.concatenate([key_parts[k] for k in range(seq_devices)], axis=0)
    value_all = jnp.concatenate([value_parts[k] for k in range(seq_devices)], axis=0)
    flat_index = slot_index.reshape(-1)
    key_slots = jnp.take(key_all, flat_index, axis=0, mode="clip").reshape(
        local_blocks, maximum_tiles, heads_here, TILE, HS
    )
    value_slots = jnp.take(value_all, flat_index, axis=0, mode="clip").reshape(
        local_blocks, maximum_tiles, heads_here, TILE, HS
    )
    query_blocks = query_rows.reshape(local_blocks, TILE, heads_here, HS)
    scores = jnp.einsum(
        "bihd,bmhjd->hbimj", query_blocks, key_slots, preferred_element_type=jnp.float32
    ) * HS ** (-0.5)
    valid_mask = my_valid[None, :, None, :, None]
    row_max = jnp.max(jnp.where(valid_mask, scores, -1e30), axis=(3, 4), keepdims=True)
    weights = jnp.where(valid_mask, jnp.exp(scores - row_max), 0.0)
    column_scale = jnp.ones(weights.shape[:2] + weights.shape[3:], jnp.float32)
    onehot = matches.astype(jnp.float32)
    for round_number in range(BALANCING_ROUNDS):
        row_scale = 1.0 / jnp.sum(weights * column_scale[:, :, None], axis=(3, 4))
        partial_cols = column_scale * jnp.sum(weights * row_scale[:, :, :, None, None], axis=2)
        column_complete = jnp.einsum(
            "bmt,hbmj->thj", onehot, partial_cols, precision=lax.Precision.HIGHEST
        ).reshape(seq_devices, local_blocks, heads_here, TILE)
        from_all = lax.all_to_all(
            column_complete, ("seq", "sub"), split_axis=0, concat_axis=0, tiled=True
        )
        owned_sums = jnp.sum(from_all, axis=0)
        spread = jnp.broadcast_to(owned_sums[None], (seq_devices,) + owned_sums.shape)
        totals = lax.all_to_all(
            spread, ("seq", "sub"), split_axis=0, concat_axis=0, tiled=True
        ).reshape(block_total, heads_here, TILE)
        per_slot = jnp.einsum("bmt,thj->hbmj", onehot, totals, precision=lax.Precision.HIGHEST)
        column_scale = column_scale / jnp.maximum(per_slot, COLUMN_FLOOR)
    probabilities = (
        weights * row_scale[:, :, :, None, None] * column_scale[:, :, None]
    ).astype(jnp.bfloat16)
    attended = jnp.einsum(
        "hbimj,bmhjd->bihd", probabilities, value_slots, preferred_element_type=jnp.float32
    )
    attended = attended.astype(jnp.bfloat16).reshape(row_count, heads_here * HS)
    head_count = lax.axis_size("head")
    if head_count != 2:
        partial_out = jnp.dot(attended, w_out, preferred_element_type=jnp.float32)
        return lax.psum_scatter(
            partial_out.astype(jnp.bfloat16), "head", scatter_dimension=1, tiled=True
        )
    head_index = lax.axis_index("head")
    width = w_out.shape[1] // 2
    other_cols = lax.dynamic_slice_in_dim(w_out, (1 - head_index) * width, width, 1)
    my_cols = lax.dynamic_slice_in_dim(w_out, head_index * width, width, 1)
    other_part = jnp.dot(attended, other_cols, preferred_element_type=jnp.float32)
    received = lax.ppermute(other_part.astype(jnp.bfloat16), "head", perm=[(0, 1), (1, 0)])
    my_part = jnp.dot(attended, my_cols, preferred_element_type=jnp.float32)
    return (my_part + received.astype(jnp.float32)).astype(jnp.bfloat16)


def solution(mesh):
    placed = (
        P(("groups", "seq", "sub"), None),
        P(None, "head"),
        P(None, "head"),
        P(None, "head"),
        P("head", None),
        P("groups", None),
        P("groups"),
    )
    return jax.shard_map(
        body,
        mesh=mesh,
        in_specs=placed,
        out_specs=P(("groups", "seq", "sub"), "head"),
        check_vma=False,
    )
```

```python
import jax
import jax.numpy as jnp
from jax import lax
from jax.sharding import PartitionSpec as P

HS = 128
TILE = 128
BALANCING_ROUNDS = 3


COLUMN_FLOOR = 0.1


def body(activations, w_query, w_key, w_value, w_out, tile_lists, query_block_counts):
    seq_devices = lax.axis_size(("seq", "sub"))
    device_index = lax.axis_index(("seq", "sub"))
    block_total = tile_lists.shape[0]
    maximum_tiles = tile_lists.shape[1]
    row_count = activations.shape[0]
    local_blocks = row_count // TILE
    heads_here = w_query.shape[1] // HS
    capacity = local_blocks * (maximum_tiles // 2) // seq_devices
    head_count = lax.axis_size("head")
    head_index = lax.axis_index("head")
    rows_part = TILE // head_count
    query_rows = jnp.dot(activations, w_query, preferred_element_type=jnp.float32).astype(
        jnp.bfloat16
    )
    act_tiles = activations.reshape(local_blocks, TILE, activations.shape[1])
    my_rows = lax.dynamic_slice_in_dim(act_tiles, head_index * rows_part, rows_part, 1)
    all_valid = jnp.arange(maximum_tiles, dtype=jnp.int32)[None, :] < query_block_counts[:, None]
    owned_ids = device_index * local_blocks + jnp.arange(local_blocks, dtype=jnp.int32)
    wanted = jnp.any(
        (tile_lists[:, :, None] == owned_ids[None, None, :]) & all_valid[:, :, None], axis=1
    )
    wanted = jnp.any(wanted.reshape(seq_devices, local_blocks, local_blocks), axis=1).astype(
        jnp.int32
    )
    slot_ranks = jnp.cumsum(wanted, axis=1) - wanted
    selector = (slot_ranks[:, None, :] == jnp.arange(capacity, dtype=jnp.int32)[None, :, None]) & (
        wanted[:, None, :] > 0
    )
    send_index = jnp.sum(
        selector.astype(jnp.int32) * jnp.arange(local_blocks, dtype=jnp.int32)[None, None, :], axis=2
    )
    my_lists = lax.dynamic_slice_in_dim(tile_lists, device_index * local_blocks, local_blocks, 0)
    my_valid = lax.dynamic_slice_in_dim(all_valid, device_index * local_blocks, local_blocks, 0)
    tile_ids = jnp.arange(block_total, dtype=jnp.int32)
    matches = (my_lists[:, :, None] == tile_ids[None, None, :]) & my_valid[:, :, None]
    requested = jnp.any(matches, axis=(0, 1)).astype(jnp.int32).reshape(seq_devices, local_blocks)
    own_ranks = jnp.cumsum(requested, axis=1) - requested
    sources = jnp.arange(seq_devices, dtype=jnp.int32)
    if seq_devices & (seq_devices - 1) == 0:
        source_steps = jnp.bitwise_xor(sources, device_index)
    else:
        source_steps = (device_index - sources) % seq_devices
    slot_table = (source_steps[:, None] * capacity + own_ranks).reshape(-1)
    slot_index = jnp.sum(jnp.where(matches, slot_table[None, None, :], 0), axis=2)
    key_weights = w_key.reshape(w_key.shape[0], heads_here, HS)
    value_weights = w_value.reshape(w_value.shape[0], heads_here, HS)
    power_of_two = seq_devices & (seq_devices - 1) == 0
    own_index = send_index[device_index]
    later_steps = jnp.arange(1, seq_devices, dtype=jnp.int32)
    if power_of_two:
        step_targets = jnp.bitwise_xor(device_index, later_steps)
    else:
        step_targets = (device_index + later_steps) % seq_devices
    step_pieces = jnp.take(
        my_rows, jnp.take(send_index, step_targets, axis=0).reshape(-1), axis=0, mode="clip"
    ).reshape(seq_devices - 1, capacity, rows_part, my_rows.shape[2])
    key_parts = {}
    value_parts = {}
    for step in sorted(range(seq_devices), key=lambda k: (k != 0, -k)):
        if step == 0:
            if head_count == 2:
                other_rows = lax.dynamic_slice_in_dim(
                    act_tiles, (1 - head_index) * rows_part, rows_part, 1
                )
                full = jnp.concatenate([my_rows, other_rows], axis=1)
            else:
                full = act_tiles
            full = jnp.take(full, own_index, axis=0, mode="clip")
        else:
            if power_of_two:
                target = jnp.bitwise_xor(device_index, step)
                pairs = [(i, i ^ step) for i in range(seq_devices)]
            else:
                target = (device_index + step) % seq_devices
                pairs = [(i, (i + step) % seq_devices) for i in range(seq_devices)]
            piece = step_pieces[step - 1]
            got = lax.ppermute(piece, ("seq", "sub"), perm=pairs)
            if head_count == 2:
                partner = lax.ppermute(got, "head", perm=[(0, 1), (1, 0)])
                full = jnp.concatenate([got, partner], axis=1)
            else:
                full = lax.all_gather(got, "head", axis=1, tiled=True)
        key_parts[step] = jnp.einsum(
            "cjf,fhd->chjd", full, key_weights, preferred_element_type=jnp.float32
        ).astype(jnp.bfloat16)
        value_parts[step] = jnp.einsum(
            "cjf,fhd->chjd", full, value_weights, preferred_element_type=jnp.float32
        ).astype(jnp.bfloat16)
    key_all = jnp.concatenate([key_parts[k] for k in range(seq_devices)], axis=0)
    value_all = jnp.concatenate([value_parts[k] for k in range(seq_devices)], axis=0)
    flat_index = slot_index.reshape(-1)
    key_slots = jnp.take(key_all, flat_index, axis=0, mode="clip").reshape(
        local_blocks, maximum_tiles, heads_here, TILE, HS
    )
    value_slots = jnp.take(value_all, flat_index, axis=0, mode="clip").reshape(
        local_blocks, maximum_tiles, heads_here, TILE, HS
    )
    query_blocks = query_rows.reshape(local_blocks, TILE, heads_here, HS)
    scores = jnp.einsum(
        "bihd,bmhjd->hbimj", query_blocks, key_slots, preferred_element_type=jnp.float32
    ) * HS ** (-0.5)
    valid_mask = my_valid[None, :, None, :, None]
    row_max = jnp.max(jnp.where(valid_mask, scores, -1e30), axis=(3, 4), keepdims=True)
    weights = jnp.where(valid_mask, jnp.exp(scores - row_max), 0.0)
    column_scale = jnp.ones(weights.shape[:2] + weights.shape[3:], jnp.float32)
    onehot = matches.astype(jnp.float32)
    for round_number in range(BALANCING_ROUNDS):
        row_scale = 1.0 / jnp.sum(weights * column_scale[:, :, None], axis=(3, 4))
        partial_cols = column_scale * jnp.sum(weights * row_scale[:, :, :, None, None], axis=2)
        column_complete = jnp.einsum(
            "bmt,hbmj->thj", onehot, partial_cols, precision=lax.Precision.HIGHEST
        ).reshape(seq_devices, local_blocks * heads_here * TILE)
        from_all = lax.all_to_all(
            column_complete, ("seq", "sub"), split_axis=0, concat_axis=0, tiled=True
        )
        owned_sums = jnp.sum(from_all, axis=0)
        spread = jnp.broadcast_to(owned_sums[None], (seq_devices,) + owned_sums.shape)
        totals = lax.all_to_all(
            spread, ("seq", "sub"), split_axis=0, concat_axis=0, tiled=True
        ).reshape(block_total, heads_here, TILE)
        per_slot = jnp.einsum("bmt,thj->hbmj", onehot, totals, precision=lax.Precision.HIGHEST)
        column_scale = column_scale / jnp.maximum(per_slot, COLUMN_FLOOR)
    probabilities = (
        weights * row_scale[:, :, :, None, None] * column_scale[:, :, None]
    ).astype(jnp.bfloat16)
    attended = jnp.einsum(
        "hbimj,bmhjd->bihd", probabilities, value_slots, preferred_element_type=jnp.float32
    )
    attended = attended.astype(jnp.bfloat16).reshape(row_count, heads_here * HS)
    head_count = lax.axis_size("head")
    if head_count != 2:
        partial_out = jnp.dot(attended, w_out, preferred_element_type=jnp.float32)
        return lax.psum_scatter(
            partial_out.astype(jnp.bfloat16), "head", scatter_dimension=1, tiled=True
        )
    head_index = lax.axis_index("head")
    width = w_out.shape[1] // 2
    other_cols = lax.dynamic_slice_in_dim(w_out, (1 - head_index) * width, width, 1)
    my_cols = lax.dynamic_slice_in_dim(w_out, head_index * width, width, 1)
    other_part = jnp.dot(attended, other_cols, preferred_element_type=jnp.float32)
    received = lax.ppermute(other_part.astype(jnp.bfloat16), "head", perm=[(0, 1), (1, 0)])
    my_part = jnp.dot(attended, my_cols, preferred_element_type=jnp.float32)
    return (my_part + received.astype(jnp.float32)).astype(jnp.bfloat16)


def solution(mesh):
    placed = (
        P(("groups", "seq", "sub"), None),
        P(None, "head"),
        P(None, "head"),
        P(None, "head"),
        P("head", None),
        P("groups", None),
        P("groups"),
    )
    return jax.shard_map(
        body,
        mesh=mesh,
        in_specs=placed,
        out_specs=P(("groups", "seq", "sub"), "head"),
        check_vma=False,
    )
```

```python
import jax
import jax.numpy as jnp
from jax import lax
from jax.sharding import PartitionSpec as P

HS = 128
TILE = 128
BALANCING_ROUNDS = 3


COLUMN_FLOOR = 0.1


def body(activations, w_query, w_key, w_value, w_out, tile_lists, query_block_counts):
    seq_devices = lax.axis_size(("seq", "sub"))
    device_index = lax.axis_index(("seq", "sub"))
    block_total = tile_lists.shape[0]
    maximum_tiles = tile_lists.shape[1]
    row_count = activations.shape[0]
    local_blocks = row_count // TILE
    heads_here = w_query.shape[1] // HS
    capacity = local_blocks * (maximum_tiles // 2) // seq_devices
    head_count = lax.axis_size("head")
    head_index = lax.axis_index("head")
    rows_part = TILE // head_count
    query_rows = jnp.dot(activations, w_query, preferred_element_type=jnp.float32).astype(
        jnp.bfloat16
    )
    act_tiles = activations.reshape(local_blocks, TILE, activations.shape[1])
    my_rows = lax.dynamic_slice_in_dim(act_tiles, head_index * rows_part, rows_part, 1)
    all_valid = jnp.arange(maximum_tiles, dtype=jnp.int32)[None, :] < query_block_counts[:, None]
    owned_ids = device_index * local_blocks + jnp.arange(local_blocks, dtype=jnp.int32)
    wanted = jnp.any(
        (tile_lists[:, :, None] == owned_ids[None, None, :]) & all_valid[:, :, None], axis=1
    )
    wanted = jnp.any(wanted.reshape(seq_devices, local_blocks, local_blocks), axis=1).astype(
        jnp.int32
    )
    slot_ranks = jnp.cumsum(wanted, axis=1) - wanted
    selector = (slot_ranks[:, None, :] == jnp.arange(capacity, dtype=jnp.int32)[None, :, None]) & (
        wanted[:, None, :] > 0
    )
    send_index = jnp.sum(
        selector.astype(jnp.int32) * jnp.arange(local_blocks, dtype=jnp.int32)[None, None, :], axis=2
    )
    my_lists = lax.dynamic_slice_in_dim(tile_lists, device_index * local_blocks, local_blocks, 0)
    my_valid = lax.dynamic_slice_in_dim(all_valid, device_index * local_blocks, local_blocks, 0)
    tile_ids = jnp.arange(block_total, dtype=jnp.int32)
    matches = (my_lists[:, :, None] == tile_ids[None, None, :]) & my_valid[:, :, None]
    requested = jnp.any(matches, axis=(0, 1)).astype(jnp.int32).reshape(seq_devices, local_blocks)
    own_ranks = jnp.cumsum(requested, axis=1) - requested
    sources = jnp.arange(seq_devices, dtype=jnp.int32)
    if seq_devices & (seq_devices - 1) == 0:
        source_steps = jnp.bitwise_xor(sources, device_index)
    else:
        source_steps = (device_index - sources) % seq_devices
    slot_table = (source_steps[:, None] * capacity + own_ranks).reshape(-1)
    slot_index = jnp.sum(jnp.where(matches, slot_table[None, None, :], 0), axis=2)
    key_weights = w_key.reshape(w_key.shape[0], heads_here, HS)
    value_weights = w_value.reshape(w_value.shape[0], heads_here, HS)
    power_of_two = seq_devices & (seq_devices - 1) == 0
    own_index = send_index[device_index]
    later_steps = jnp.arange(1, seq_devices, dtype=jnp.int32)
    if power_of_two:
        step_targets = jnp.bitwise_xor(device_index, later_steps)
    else:
        step_targets = (device_index + later_steps) % seq_devices
    step_pieces = jnp.take(
        my_rows, jnp.take(send_index, step_targets, axis=0).reshape(-1), axis=0, mode="clip"
    ).reshape(seq_devices - 1, capacity, rows_part, my_rows.shape[2])
    key_parts = {}
    value_parts = {}
    for step in sorted(range(seq_devices), key=lambda k: (k != 0, -k)):
        if step == 0:
            if head_count == 2:
                other_rows = lax.dynamic_slice_in_dim(
                    act_tiles, (1 - head_index) * rows_part, rows_part, 1
                )
                full = jnp.concatenate([my_rows, other_rows], axis=1)
            else:
                full = act_tiles
            full = jnp.take(full, own_index, axis=0, mode="clip")
        else:
            if power_of_two:
                target = jnp.bitwise_xor(device_index, step)
                pairs = [(i, i ^ step) for i in range(seq_devices)]
            else:
                target = (device_index + step) % seq_devices
                pairs = [(i, (i + step) % seq_devices) for i in range(seq_devices)]
            piece = step_pieces[step - 1]
            got = lax.ppermute(piece, ("seq", "sub"), perm=pairs)
            if head_count == 2:
                partner = lax.ppermute(got, "head", perm=[(0, 1), (1, 0)])
                full = jnp.concatenate([got, partner], axis=1)
            else:
                full = lax.all_gather(got, "head", axis=1, tiled=True)
        key_parts[step] = jnp.einsum(
            "cjf,fhd->chjd", full, key_weights, preferred_element_type=jnp.float32
        ).astype(jnp.bfloat16)
        value_parts[step] = jnp.einsum(
            "cjf,fhd->chjd", full, value_weights, preferred_element_type=jnp.float32
        ).astype(jnp.bfloat16)
    key_all = jnp.concatenate([key_parts[k] for k in range(seq_devices)], axis=0)
    value_all = jnp.concatenate([value_parts[k] for k in range(seq_devices)], axis=0)
    flat_index = slot_index.reshape(-1)
    key_slots = jnp.take(key_all, flat_index, axis=0, mode="clip").reshape(
        local_blocks, maximum_tiles, heads_here, TILE, HS
    )
    value_slots = jnp.take(value_all, flat_index, axis=0, mode="clip").reshape(
        local_blocks, maximum_tiles, heads_here, TILE, HS
    )
    query_blocks = query_rows.reshape(local_blocks, TILE, heads_here, HS)
    scores = jnp.einsum(
        "bihd,bmhjd->hbimj", query_blocks, key_slots, preferred_element_type=jnp.float32
    ) * HS ** (-0.5)
    valid_mask = my_valid[None, :, None, :, None]
    row_max = jnp.max(jnp.where(valid_mask, scores, -1e30), axis=(3, 4), keepdims=True)
    weights = jnp.where(valid_mask, jnp.exp(scores - row_max), 0.0)
    column_scale = jnp.ones(weights.shape[:2] + weights.shape[3:], jnp.float32)
    onehot = matches.astype(jnp.float32)
    for round_number in range(BALANCING_ROUNDS):
        row_scale = 1.0 / jnp.sum(weights * column_scale[:, :, None], axis=(3, 4))
        partial_cols = column_scale * jnp.sum(weights * row_scale[:, :, :, None, None], axis=2)
        column_complete = jnp.einsum(
            "bmt,hbmj->thj", onehot, partial_cols, precision=lax.Precision.HIGHEST
        ).reshape(seq_devices, local_blocks, heads_here, TILE)
        from_all = lax.all_to_all(
            column_complete, ("seq", "sub"), split_axis=0, concat_axis=0, tiled=True
        )
        owned_sums = jnp.sum(from_all, axis=0)
        spread = jnp.broadcast_to(owned_sums[None], (seq_devices,) + owned_sums.shape)
        totals = lax.all_to_all(
            spread, ("seq", "sub"), split_axis=0, concat_axis=0, tiled=True
        ).reshape(block_total, heads_here, TILE)
        per_slot = jnp.einsum("bmt,thj->hbmj", onehot, totals, precision=lax.Precision.HIGHEST)
        column_scale = column_scale / jnp.maximum(per_slot, COLUMN_FLOOR)
    probabilities = (
        weights * row_scale[:, :, :, None, None] * column_scale[:, :, None]
    ).astype(jnp.bfloat16)
    head_count = lax.axis_size("head")
    if head_count != 2 or heads_here % 2 != 0:
        attended = jnp.einsum(
            "hbimj,bmhjd->bihd", probabilities, value_slots, preferred_element_type=jnp.float32
        )
        attended = attended.astype(jnp.bfloat16).reshape(row_count, heads_here * HS)
        partial_out = jnp.dot(attended, w_out, preferred_element_type=jnp.float32)
        return lax.psum_scatter(
            partial_out.astype(jnp.bfloat16), "head", scatter_dimension=1, tiled=True
        )
    head_index = lax.axis_index("head")
    width = w_out.shape[1] // 2
    swap = [(0, 1), (1, 0)]
    my_cols = lax.dynamic_slice_in_dim(w_out, head_index * width, width, 1)
    partner_rows = lax.ppermute(
        lax.dynamic_slice_in_dim(w_out, (1 - head_index) * width, width, 1), "head", perm=swap
    )
    group = heads_here // 2
    total = None
    for group_number in range(2):
        first = group_number * group
        attended = jnp.einsum(
            "hbimj,bmhjd->bihd",
            probabilities[first : first + group],
            value_slots[:, :, first : first + group],
            preferred_element_type=jnp.float32,
        )
        attended = attended.astype(jnp.bfloat16).reshape(row_count, group * HS)
        received = lax.ppermute(attended, "head", perm=swap)
        rows = slice(first * HS, (first + group) * HS)
        part = jnp.dot(attended, my_cols[rows], preferred_element_type=jnp.float32) + jnp.dot(
            received, partner_rows[rows], preferred_element_type=jnp.float32
        )
        total = part if total is None else total + part
    return total.astype(jnp.bfloat16)


def solution(mesh):
    placed = (
        P(("groups", "seq", "sub"), None),
        P(None, "head"),
        P(None, "head"),
        P(None, "head"),
        P("head", None),
        P("groups", None),
        P("groups"),
    )
    return jax.shard_map(
        body,
        mesh=mesh,
        in_specs=placed,
        out_specs=P(("groups", "seq", "sub"), "head"),
        check_vma=False,
    )
```

```python
import jax
import jax.numpy as jnp
from jax import lax
from jax.sharding import PartitionSpec as P

HS = 128
TILE = 128
BALANCING_ROUNDS = 3


COLUMN_FLOOR = 0.1


def body(activations, w_query, w_key, w_value, w_out, tile_lists, query_block_counts):
    seq_devices = lax.axis_size(("seq", "sub"))
    device_index = lax.axis_index(("seq", "sub"))
    block_total = tile_lists.shape[0]
    maximum_tiles = tile_lists.shape[1]
    row_count = activations.shape[0]
    local_blocks = row_count // TILE
    heads_here = w_query.shape[1] // HS
    capacity = local_blocks * (maximum_tiles // 2) // seq_devices
    head_count = lax.axis_size("head")
    head_index = lax.axis_index("head")
    rows_part = TILE // head_count
    query_rows = jnp.dot(activations, w_query, preferred_element_type=jnp.float32).astype(
        jnp.bfloat16
    )
    act_tiles = activations.reshape(local_blocks, TILE, activations.shape[1])
    my_rows = lax.dynamic_slice_in_dim(act_tiles, head_index * rows_part, rows_part, 1)
    all_valid = jnp.arange(maximum_tiles, dtype=jnp.int32)[None, :] < query_block_counts[:, None]
    owned_ids = device_index * local_blocks + jnp.arange(local_blocks, dtype=jnp.int32)
    wanted = jnp.any(
        (tile_lists[:, :, None] == owned_ids[None, None, :]) & all_valid[:, :, None], axis=1
    )
    wanted = jnp.any(wanted.reshape(seq_devices, local_blocks, local_blocks), axis=1).astype(
        jnp.int32
    )
    slot_ranks = jnp.cumsum(wanted, axis=1) - wanted
    selector = (slot_ranks[:, None, :] == jnp.arange(capacity, dtype=jnp.int32)[None, :, None]) & (
        wanted[:, None, :] > 0
    )
    send_index = jnp.sum(
        selector.astype(jnp.int32) * jnp.arange(local_blocks, dtype=jnp.int32)[None, None, :], axis=2
    )
    my_lists = lax.dynamic_slice_in_dim(tile_lists, device_index * local_blocks, local_blocks, 0)
    my_valid = lax.dynamic_slice_in_dim(all_valid, device_index * local_blocks, local_blocks, 0)
    tile_ids = jnp.arange(block_total, dtype=jnp.int32)
    matches = (my_lists[:, :, None] == tile_ids[None, None, :]) & my_valid[:, :, None]
    requested = jnp.any(matches, axis=(0, 1)).astype(jnp.int32).reshape(seq_devices, local_blocks)
    own_ranks = jnp.cumsum(requested, axis=1) - requested
    sources = jnp.arange(seq_devices, dtype=jnp.int32)
    if seq_devices & (seq_devices - 1) == 0:
        source_steps = jnp.bitwise_xor(sources, device_index)
    else:
        source_steps = (device_index - sources) % seq_devices
    slot_table = (source_steps[:, None] * capacity + own_ranks).reshape(-1)
    slot_index = jnp.sum(jnp.where(matches, slot_table[None, None, :], 0), axis=2)
    key_weights = w_key.reshape(w_key.shape[0], heads_here, HS)
    value_weights = w_value.reshape(w_value.shape[0], heads_here, HS)
    power_of_two = seq_devices & (seq_devices - 1) == 0
    own_index = send_index[device_index]
    later_steps = jnp.arange(1, seq_devices, dtype=jnp.int32)
    if power_of_two:
        step_targets = jnp.bitwise_xor(device_index, later_steps)
    else:
        step_targets = (device_index + later_steps) % seq_devices
    step_pieces = jnp.take(
        my_rows, jnp.take(send_index, step_targets, axis=0).reshape(-1), axis=0, mode="clip"
    ).reshape(seq_devices - 1, capacity, rows_part, my_rows.shape[2])
    key_parts = {}
    value_parts = {}
    for step in sorted(range(seq_devices), key=lambda k: (k != 0, -k)):
        if step == 0:
            if head_count == 2:
                other_rows = lax.dynamic_slice_in_dim(
                    act_tiles, (1 - head_index) * rows_part, rows_part, 1
                )
                full = jnp.concatenate([my_rows, other_rows], axis=1)
            else:
                full = act_tiles
            full = jnp.take(full, own_index, axis=0, mode="clip")
        else:
            if power_of_two:
                target = jnp.bitwise_xor(device_index, step)
                pairs = [(i, i ^ step) for i in range(seq_devices)]
            else:
                target = (device_index + step) % seq_devices
                pairs = [(i, (i + step) % seq_devices) for i in range(seq_devices)]
            piece = step_pieces[step - 1]
            got = lax.ppermute(piece, ("seq", "sub"), perm=pairs)
            if head_count == 2:
                partner = lax.ppermute(got, "head", perm=[(0, 1), (1, 0)])
                full = jnp.concatenate([got, partner], axis=1)
            else:
                full = lax.all_gather(got, "head", axis=1, tiled=True)
        key_parts[step] = jnp.einsum(
            "cjf,fhd->chjd", full, key_weights, preferred_element_type=jnp.float32
        ).astype(jnp.bfloat16)
        value_parts[step] = jnp.einsum(
            "cjf,fhd->chjd", full, value_weights, preferred_element_type=jnp.float32
        ).astype(jnp.bfloat16)
    key_all = jnp.concatenate([key_parts[k] for k in range(seq_devices)], axis=0)
    value_all = jnp.concatenate([value_parts[k] for k in range(seq_devices)], axis=0)
    flat_index = slot_index.reshape(-1)
    key_slots = jnp.take(key_all, flat_index, axis=0, mode="clip").reshape(
        local_blocks, maximum_tiles, heads_here, TILE, HS
    )
    value_slots = jnp.take(value_all, flat_index, axis=0, mode="clip").reshape(
        local_blocks, maximum_tiles, heads_here, TILE, HS
    )
    query_blocks = query_rows.reshape(local_blocks, TILE, heads_here, HS)
    scores = jnp.einsum(
        "bihd,bmhjd->hbimj", query_blocks, key_slots, preferred_element_type=jnp.float32
    ) * HS ** (-0.5)
    valid_mask = my_valid[None, :, None, :, None]
    row_max = jnp.max(jnp.where(valid_mask, scores, -1e30), axis=(3, 4), keepdims=True)
    weights = jnp.where(valid_mask, jnp.exp(scores - row_max), 0.0)
    column_scale = jnp.ones(weights.shape[:2] + weights.shape[3:], jnp.float32)
    onehot = matches.astype(jnp.float32)
    for round_number in range(BALANCING_ROUNDS):
        row_scale = 1.0 / jnp.sum(weights * column_scale[:, :, None], axis=(3, 4))
        partial_cols = column_scale * jnp.sum(weights * row_scale[:, :, :, None, None], axis=2)
        column_complete = jnp.einsum(
            "bmt,hbmj->thj", onehot, partial_cols, precision=lax.Precision.HIGHEST
        ).reshape(seq_devices, local_blocks, heads_here, TILE)
        from_all = lax.all_to_all(
            column_complete, ("seq", "sub"), split_axis=0, concat_axis=0, tiled=True
        )
        owned_sums = jnp.sum(from_all, axis=0)
        spread = jnp.broadcast_to(owned_sums[None], (seq_devices,) + owned_sums.shape)
        totals = lax.all_to_all(
            spread, ("seq", "sub"), split_axis=0, concat_axis=0, tiled=True
        ).reshape(block_total, heads_here, TILE)
        per_slot = jnp.einsum("bmt,thj->hbmj", onehot, totals, precision=lax.Precision.HIGHEST)
        column_scale = column_scale / jnp.maximum(per_slot, COLUMN_FLOOR)
    probabilities = (
        weights * row_scale[:, :, :, None, None] * column_scale[:, :, None]
    ).astype(jnp.bfloat16)
    head_count = lax.axis_size("head")
    if head_count != 2 or heads_here % 2 != 0:
        attended = jnp.einsum(
            "hbimj,bmhjd->bihd", probabilities, value_slots, preferred_element_type=jnp.float32
        )
        attended = attended.astype(jnp.bfloat16).reshape(row_count, heads_here * HS)
        partial_out = jnp.dot(attended, w_out, preferred_element_type=jnp.float32)
        return lax.psum_scatter(
            partial_out.astype(jnp.bfloat16), "head", scatter_dimension=1, tiled=True
        )
    head_index = lax.axis_index("head")
    width = w_out.shape[1] // 2
    swap = [(0, 1), (1, 0)]
    my_cols = lax.dynamic_slice_in_dim(w_out, head_index * width, width, 1)
    partner_rows = lax.ppermute(
        lax.dynamic_slice_in_dim(w_out, (1 - head_index) * width, width, 1), "head", perm=swap
    )
    group = heads_here // 2
    total = None
    previous = None
    for group_number in range(2):
        first = group_number * group
        group_rows = row_scale[first : first + group]
        if previous is not None:
            group_rows, _ = lax.optimization_barrier((group_rows, previous))
        group_probabilities = (
            weights[first : first + group]
            * group_rows[:, :, :, None, None]
            * column_scale[first : first + group, :, None]
        ).astype(jnp.bfloat16)
        attended = jnp.einsum(
            "hbimj,bmhjd->bihd",
            group_probabilities,
            value_slots[:, :, first : first + group],
            preferred_element_type=jnp.float32,
        )
        attended = attended.astype(jnp.bfloat16).reshape(row_count, group * HS)
        previous = attended
        received = lax.ppermute(attended, "head", perm=swap)
        rows = slice(first * HS, (first + group) * HS)
        part = jnp.dot(attended, my_cols[rows], preferred_element_type=jnp.float32) + jnp.dot(
            received, partner_rows[rows], preferred_element_type=jnp.float32
        )
        total = part if total is None else total + part
    return total.astype(jnp.bfloat16)


def solution(mesh):
    placed = (
        P(("groups", "seq", "sub"), None),
        P(None, "head"),
        P(None, "head"),
        P(None, "head"),
        P("head", None),
        P("groups", None),
        P("groups"),
    )
    return jax.shard_map(
        body,
        mesh=mesh,
        in_specs=placed,
        out_specs=P(("groups", "seq", "sub"), "head"),
        check_vma=False,
    )
```

```python
import jax
import jax.numpy as jnp
from jax import lax
from jax.sharding import PartitionSpec as P

HS = 128
TILE = 128
BALANCING_ROUNDS = 3


COLUMN_FLOOR = 0.1


def body(activations, w_query, w_key, w_value, w_out, tile_lists, query_block_counts):
    seq_devices = lax.axis_size(("seq", "sub"))
    device_index = lax.axis_index(("seq", "sub"))
    block_total = tile_lists.shape[0]
    maximum_tiles = tile_lists.shape[1]
    row_count = activations.shape[0]
    local_blocks = row_count // TILE
    heads_here = w_query.shape[1] // HS
    capacity = local_blocks * (maximum_tiles // 2) // seq_devices
    head_count = lax.axis_size("head")
    head_index = lax.axis_index("head")
    rows_part = TILE // head_count
    query_rows = jnp.dot(activations, w_query, preferred_element_type=jnp.float32).astype(
        jnp.bfloat16
    )
    act_tiles = activations.reshape(local_blocks, TILE, activations.shape[1])
    my_rows = lax.dynamic_slice_in_dim(act_tiles, head_index * rows_part, rows_part, 1)
    all_valid = jnp.arange(maximum_tiles, dtype=jnp.int32)[None, :] < query_block_counts[:, None]
    owned_ids = device_index * local_blocks + jnp.arange(local_blocks, dtype=jnp.int32)
    wanted = jnp.any(
        (tile_lists[:, :, None] == owned_ids[None, None, :]) & all_valid[:, :, None], axis=1
    )
    wanted = jnp.any(wanted.reshape(seq_devices, local_blocks, local_blocks), axis=1).astype(
        jnp.int32
    )
    slot_ranks = jnp.cumsum(wanted, axis=1) - wanted
    selector = (slot_ranks[:, None, :] == jnp.arange(capacity, dtype=jnp.int32)[None, :, None]) & (
        wanted[:, None, :] > 0
    )
    send_index = jnp.sum(
        selector.astype(jnp.int32) * jnp.arange(local_blocks, dtype=jnp.int32)[None, None, :], axis=2
    )
    my_lists = lax.dynamic_slice_in_dim(tile_lists, device_index * local_blocks, local_blocks, 0)
    my_valid = lax.dynamic_slice_in_dim(all_valid, device_index * local_blocks, local_blocks, 0)
    tile_ids = jnp.arange(block_total, dtype=jnp.int32)
    matches = (my_lists[:, :, None] == tile_ids[None, None, :]) & my_valid[:, :, None]
    requested = jnp.any(matches, axis=(0, 1)).astype(jnp.int32).reshape(seq_devices, local_blocks)
    own_ranks = jnp.cumsum(requested, axis=1) - requested
    sources = jnp.arange(seq_devices, dtype=jnp.int32)
    if seq_devices & (seq_devices - 1) == 0:
        source_steps = jnp.bitwise_xor(sources, device_index)
    else:
        source_steps = (device_index - sources) % seq_devices
    slot_table = (source_steps[:, None] * capacity + own_ranks).reshape(-1)
    slot_index = jnp.sum(jnp.where(matches, slot_table[None, None, :], 0), axis=2)
    key_weights = w_key.reshape(w_key.shape[0], heads_here, HS)
    value_weights = w_value.reshape(w_value.shape[0], heads_here, HS)
    power_of_two = seq_devices & (seq_devices - 1) == 0
    own_index = send_index[device_index]
    later_steps = jnp.arange(1, seq_devices, dtype=jnp.int32)
    if power_of_two:
        step_targets = jnp.bitwise_xor(device_index, later_steps)
    else:
        step_targets = (device_index + later_steps) % seq_devices
    step_pieces = jnp.take(
        my_rows, jnp.take(send_index, step_targets, axis=0).reshape(-1), axis=0, mode="clip"
    ).reshape(seq_devices - 1, capacity, rows_part, my_rows.shape[2])
    key_parts = {}
    value_parts = {}
    for step in sorted(range(seq_devices), key=lambda k: (k != 0, -k)):
        if step == 0:
            if head_count == 2:
                other_rows = lax.dynamic_slice_in_dim(
                    act_tiles, (1 - head_index) * rows_part, rows_part, 1
                )
                full = jnp.concatenate([my_rows, other_rows], axis=1)
            else:
                full = act_tiles
            full = jnp.take(full, own_index, axis=0, mode="clip")
        else:
            if power_of_two:
                target = jnp.bitwise_xor(device_index, step)
                pairs = [(i, i ^ step) for i in range(seq_devices)]
            else:
                target = (device_index + step) % seq_devices
                pairs = [(i, (i + step) % seq_devices) for i in range(seq_devices)]
            piece = step_pieces[step - 1]
            got = lax.ppermute(piece, ("seq", "sub"), perm=pairs)
            if head_count == 2:
                partner = lax.ppermute(got, "head", perm=[(0, 1), (1, 0)])
                full = jnp.concatenate([got, partner], axis=1)
            else:
                full = lax.all_gather(got, "head", axis=1, tiled=True)
        key_parts[step] = jnp.einsum(
            "cjf,fhd->chjd", full, key_weights, preferred_element_type=jnp.float32
        ).astype(jnp.bfloat16)
        value_parts[step] = jnp.einsum(
            "cjf,fhd->chjd", full, value_weights, preferred_element_type=jnp.float32
        ).astype(jnp.bfloat16)
    key_all = jnp.concatenate([key_parts[k] for k in range(seq_devices)], axis=0)
    value_all = jnp.concatenate([value_parts[k] for k in range(seq_devices)], axis=0)
    flat_index = slot_index.reshape(-1)
    key_slots = jnp.take(key_all, flat_index, axis=0, mode="clip").reshape(
        local_blocks, maximum_tiles, heads_here, TILE, HS
    )
    value_slots = jnp.take(value_all, flat_index, axis=0, mode="clip").reshape(
        local_blocks, maximum_tiles, heads_here, TILE, HS
    )
    query_blocks = query_rows.reshape(local_blocks, TILE, heads_here, HS)
    scores = jnp.einsum(
        "bihd,bmhjd->hbimj", query_blocks, key_slots, preferred_element_type=jnp.float32
    ) * HS ** (-0.5)
    valid_mask = my_valid[None, :, None, :, None]
    row_max = jnp.max(jnp.where(valid_mask, scores, -1e30), axis=(3, 4), keepdims=True)
    weights = jnp.where(valid_mask, jnp.exp(scores - row_max), 0.0)
    column_scale = jnp.ones(weights.shape[:2] + weights.shape[3:], jnp.float32)
    onehot = matches.astype(jnp.float32)
    for round_number in range(BALANCING_ROUNDS):
        row_scale = 1.0 / jnp.sum(weights * column_scale[:, :, None], axis=(3, 4))
        partial_cols = column_scale * jnp.sum(weights * row_scale[:, :, :, None, None], axis=2)
        column_complete = jnp.einsum(
            "bmt,hbmj->thj", onehot, partial_cols, precision=lax.Precision.HIGHEST
        ).reshape(seq_devices, local_blocks, heads_here, TILE)
        from_all = lax.all_to_all(
            column_complete, ("seq", "sub"), split_axis=0, concat_axis=0, tiled=True
        )
        owned_sums = jnp.sum(from_all, axis=0)
        spread = jnp.broadcast_to(owned_sums[None], (seq_devices,) + owned_sums.shape)
        totals = lax.all_to_all(
            spread, ("seq", "sub"), split_axis=0, concat_axis=0, tiled=True
        ).reshape(block_total, heads_here, TILE)
        per_slot = jnp.einsum("bmt,thj->hbmj", onehot, totals, precision=lax.Precision.HIGHEST)
        column_scale = column_scale / jnp.maximum(per_slot, COLUMN_FLOOR)
    probabilities = (
        weights * row_scale[:, :, :, None, None] * column_scale[:, :, None]
    ).astype(jnp.bfloat16)
    head_count = lax.axis_size("head")
    if head_count != 2 or heads_here % 2 != 0:
        attended = jnp.einsum(
            "hbimj,bmhjd->bihd", probabilities, value_slots, preferred_element_type=jnp.float32
        )
        attended = attended.astype(jnp.bfloat16).reshape(row_count, heads_here * HS)
        partial_out = jnp.dot(attended, w_out, preferred_element_type=jnp.float32)
        return lax.psum_scatter(
            partial_out.astype(jnp.bfloat16), "head", scatter_dimension=1, tiled=True
        )
    head_index = lax.axis_index("head")
    width = w_out.shape[1] // 2
    swap = [(0, 1), (1, 0)]
    my_cols = lax.dynamic_slice_in_dim(w_out, head_index * width, width, 1)
    partner_rows = lax.ppermute(
        lax.dynamic_slice_in_dim(w_out, (1 - head_index) * width, width, 1), "head", perm=swap
    )
    group_count = 4 if heads_here % 4 == 0 else 2
    group = heads_here // group_count
    total = None
    previous = None
    for group_number in range(group_count):
        first = group_number * group
        group_rows = row_scale[first : first + group]
        if previous is not None:
            group_rows, _ = lax.optimization_barrier((group_rows, previous))
        group_probabilities = (
            weights[first : first + group]
            * group_rows[:, :, :, None, None]
            * column_scale[first : first + group, :, None]
        ).astype(jnp.bfloat16)
        attended = jnp.einsum(
            "hbimj,bmhjd->bihd",
            group_probabilities,
            value_slots[:, :, first : first + group],
            preferred_element_type=jnp.float32,
        )
        attended = attended.astype(jnp.bfloat16).reshape(row_count, group * HS)
        previous = attended
        received = lax.ppermute(attended, "head", perm=swap)
        rows = slice(first * HS, (first + group) * HS)
        part = jnp.dot(attended, my_cols[rows], preferred_element_type=jnp.float32) + jnp.dot(
            received, partner_rows[rows], preferred_element_type=jnp.float32
        )
        total = part if total is None else total + part
    return total.astype(jnp.bfloat16)


def solution(mesh):
    placed = (
        P(("groups", "seq", "sub"), None),
        P(None, "head"),
        P(None, "head"),
        P(None, "head"),
        P("head", None),
        P("groups", None),
        P("groups"),
    )
    return jax.shard_map(
        body,
        mesh=mesh,
        in_specs=placed,
        out_specs=P(("groups", "seq", "sub"), "head"),
        check_vma=False,
    )
```

```python
import jax
import jax.numpy as jnp
from jax import lax
from jax.sharding import PartitionSpec as P

HS = 128
TILE = 128
BALANCING_ROUNDS = 3


COLUMN_FLOOR = 0.1


def body(activations, w_query, w_key, w_value, w_out, tile_lists, query_block_counts):
    seq_devices = lax.axis_size(("seq", "sub"))
    device_index = lax.axis_index(("seq", "sub"))
    block_total = tile_lists.shape[0]
    maximum_tiles = tile_lists.shape[1]
    row_count = activations.shape[0]
    local_blocks = row_count // TILE
    heads_here = w_query.shape[1] // HS
    capacity = local_blocks * (maximum_tiles // 2) // seq_devices
    head_count = lax.axis_size("head")
    head_index = lax.axis_index("head")
    rows_part = TILE // head_count
    query_rows = jnp.dot(activations, w_query, preferred_element_type=jnp.float32).astype(
        jnp.bfloat16
    )
    act_tiles = activations.reshape(local_blocks, TILE, activations.shape[1])
    my_rows = lax.dynamic_slice_in_dim(act_tiles, head_index * rows_part, rows_part, 1)
    all_valid = jnp.arange(maximum_tiles, dtype=jnp.int32)[None, :] < query_block_counts[:, None]
    owned_ids = device_index * local_blocks + jnp.arange(local_blocks, dtype=jnp.int32)
    wanted = jnp.any(
        (tile_lists[:, :, None] == owned_ids[None, None, :]) & all_valid[:, :, None], axis=1
    )
    wanted = jnp.any(wanted.reshape(seq_devices, local_blocks, local_blocks), axis=1).astype(
        jnp.int32
    )
    slot_ranks = jnp.cumsum(wanted, axis=1) - wanted
    selector = (slot_ranks[:, None, :] == jnp.arange(capacity, dtype=jnp.int32)[None, :, None]) & (
        wanted[:, None, :] > 0
    )
    send_index = jnp.sum(
        selector.astype(jnp.int32) * jnp.arange(local_blocks, dtype=jnp.int32)[None, None, :], axis=2
    )
    my_lists = lax.dynamic_slice_in_dim(tile_lists, device_index * local_blocks, local_blocks, 0)
    my_valid = lax.dynamic_slice_in_dim(all_valid, device_index * local_blocks, local_blocks, 0)
    tile_ids = jnp.arange(block_total, dtype=jnp.int32)
    matches = (my_lists[:, :, None] == tile_ids[None, None, :]) & my_valid[:, :, None]
    requested = jnp.any(matches, axis=(0, 1)).astype(jnp.int32).reshape(seq_devices, local_blocks)
    own_ranks = jnp.cumsum(requested, axis=1) - requested
    sources = jnp.arange(seq_devices, dtype=jnp.int32)
    if seq_devices & (seq_devices - 1) == 0:
        source_steps = jnp.bitwise_xor(sources, device_index)
    else:
        source_steps = (device_index - sources) % seq_devices
    slot_table = (source_steps[:, None] * capacity + own_ranks).reshape(-1)
    slot_index = jnp.sum(jnp.where(matches, slot_table[None, None, :], 0), axis=2)
    key_weights = w_key.reshape(w_key.shape[0], heads_here, HS)
    value_weights = w_value.reshape(w_value.shape[0], heads_here, HS)
    power_of_two = seq_devices & (seq_devices - 1) == 0
    own_index = send_index[device_index]
    later_steps = jnp.arange(1, seq_devices, dtype=jnp.int32)
    if power_of_two:
        step_targets = jnp.bitwise_xor(device_index, later_steps)
    else:
        step_targets = (device_index + later_steps) % seq_devices
    step_pieces = jnp.take(
        my_rows, jnp.take(send_index, step_targets, axis=0).reshape(-1), axis=0, mode="clip"
    ).reshape(seq_devices - 1, capacity, rows_part, my_rows.shape[2])
    key_parts = {}
    value_parts = {}
    for step in sorted(range(seq_devices), key=lambda k: (k != 0, -k)):
        if step == 0:
            if head_count == 2:
                other_rows = lax.dynamic_slice_in_dim(
                    act_tiles, (1 - head_index) * rows_part, rows_part, 1
                )
                full = jnp.concatenate([my_rows, other_rows], axis=1)
            else:
                full = act_tiles
            full = jnp.take(full, own_index, axis=0, mode="clip")
        else:
            if power_of_two:
                target = jnp.bitwise_xor(device_index, step)
                pairs = [(i, i ^ step) for i in range(seq_devices)]
            else:
                target = (device_index + step) % seq_devices
                pairs = [(i, (i + step) % seq_devices) for i in range(seq_devices)]
            piece = step_pieces[step - 1]
            got = lax.ppermute(piece, ("seq", "sub"), perm=pairs)
            if head_count == 2:
                partner = lax.ppermute(got, "head", perm=[(0, 1), (1, 0)])
                full = jnp.concatenate([got, partner], axis=1)
            else:
                full = lax.all_gather(got, "head", axis=1, tiled=True)
        key_parts[step] = jnp.einsum(
            "cjf,fhd->chjd", full, key_weights, preferred_element_type=jnp.float32
        ).astype(jnp.bfloat16)
        value_parts[step] = jnp.einsum(
            "cjf,fhd->chjd", full, value_weights, preferred_element_type=jnp.float32
        ).astype(jnp.bfloat16)
    key_all = jnp.concatenate([key_parts[k] for k in range(seq_devices)], axis=0)
    value_all = jnp.concatenate([value_parts[k] for k in range(seq_devices)], axis=0)
    flat_index = slot_index.reshape(-1)
    key_slots = jnp.take(key_all, flat_index, axis=0, mode="clip").reshape(
        local_blocks, maximum_tiles, heads_here, TILE, HS
    )
    value_slots = jnp.take(value_all, flat_index, axis=0, mode="clip").reshape(
        local_blocks, maximum_tiles, heads_here, TILE, HS
    )
    query_blocks = query_rows.reshape(local_blocks, TILE, heads_here, HS)
    scores = jnp.einsum(
        "bihd,bmhjd->hbimj", query_blocks, key_slots, preferred_element_type=jnp.float32
    ) * HS ** (-0.5)
    valid_mask = my_valid[None, :, None, :, None]
    row_max = jnp.max(jnp.where(valid_mask, scores, -1e30), axis=(3, 4), keepdims=True)
    weights = jnp.where(valid_mask, jnp.exp(scores - row_max), 0.0)
    column_scale = jnp.ones(weights.shape[:2] + weights.shape[3:], jnp.float32)
    onehot = matches.astype(jnp.float32)
    for round_number in range(BALANCING_ROUNDS):
        row_scale = 1.0 / jnp.sum(weights * column_scale[:, :, None], axis=(3, 4))
        partial_cols = column_scale * jnp.sum(weights * row_scale[:, :, :, None, None], axis=2)
        column_complete = jnp.einsum(
            "bmt,hbmj->thj", onehot, partial_cols, precision=lax.Precision.HIGHEST
        ).reshape(seq_devices, local_blocks, heads_here, TILE)
        from_all = lax.all_to_all(
            column_complete, ("seq", "sub"), split_axis=0, concat_axis=0, tiled=True
        )
        owned_sums = jnp.sum(from_all, axis=0)
        spread = jnp.broadcast_to(owned_sums[None], (seq_devices,) + owned_sums.shape)
        totals = lax.all_to_all(
            spread, ("seq", "sub"), split_axis=0, concat_axis=0, tiled=True
        ).reshape(block_total, heads_here, TILE)
        per_slot = jnp.einsum("bmt,thj->hbmj", onehot, totals, precision=lax.Precision.HIGHEST)
        column_scale = column_scale / jnp.maximum(per_slot, COLUMN_FLOOR)
    probabilities = (
        weights * row_scale[:, :, :, None, None] * column_scale[:, :, None]
    ).astype(jnp.bfloat16)
    head_count = lax.axis_size("head")
    if head_count != 2 or heads_here % 2 != 0:
        attended = jnp.einsum(
            "hbimj,bmhjd->bihd", probabilities, value_slots, preferred_element_type=jnp.float32
        )
        attended = attended.astype(jnp.bfloat16).reshape(row_count, heads_here * HS)
        partial_out = jnp.dot(attended, w_out, preferred_element_type=jnp.float32)
        return lax.psum_scatter(
            partial_out.astype(jnp.bfloat16), "head", scatter_dimension=1, tiled=True
        )
    head_index = lax.axis_index("head")
    width = w_out.shape[1] // 2
    swap = [(0, 1), (1, 0)]
    my_cols = lax.dynamic_slice_in_dim(w_out, head_index * width, width, 1)
    partner_rows = lax.ppermute(
        lax.dynamic_slice_in_dim(w_out, (1 - head_index) * width, width, 1), "head", perm=swap
    )
    group_count = 4 if heads_here % 4 == 0 else 2
    group = heads_here // group_count
    total = None
    previous = None
    arrivals = []
    for group_number in range(group_count):
        first = group_number * group
        group_rows = row_scale[first : first + group]
        if previous is not None:
            group_rows, _ = lax.optimization_barrier((group_rows, previous))
        group_probabilities = (
            weights[first : first + group]
            * group_rows[:, :, :, None, None]
            * column_scale[first : first + group, :, None]
        ).astype(jnp.bfloat16)
        attended = jnp.einsum(
            "hbimj,bmhjd->bihd",
            group_probabilities,
            value_slots[:, :, first : first + group],
            preferred_element_type=jnp.float32,
        )
        attended = attended.astype(jnp.bfloat16).reshape(row_count, group * HS)
        previous = attended
        arrivals.append(lax.ppermute(attended, "head", perm=swap))
        rows = slice(first * HS, (first + group) * HS)
        part = jnp.dot(attended, my_cols[rows], preferred_element_type=jnp.float32)
        total = part if total is None else total + part
    total = total + jnp.dot(
        jnp.concatenate(arrivals, axis=1), partner_rows, preferred_element_type=jnp.float32
    )
    return total.astype(jnp.bfloat16)


def solution(mesh):
    placed = (
        P(("groups", "seq", "sub"), None),
        P(None, "head"),
        P(None, "head"),
        P(None, "head"),
        P("head", None),
        P("groups", None),
        P("groups"),
    )
    return jax.shard_map(
        body,
        mesh=mesh,
        in_specs=placed,
        out_specs=P(("groups", "seq", "sub"), "head"),
        check_vma=False,
    )
```
